128 devices in a mesh: wide: 64 (over z, y, x), narrow: 2 (over core).
Axes of the slice: x: 4, y: 4, z: 4, core: 2. Of those that a mesh axis runs over, the one named last changes fastest.
Arguments:
- tokens: bfloat16 [65536, 2048], P('wide', 'narrow'), may hold values from -6 to 6
- attn_gain: bfloat16 [2048], replicated, may hold values from 0.5 to 1.5
- q_weight: bfloat16 [2048, 3072], P('wide', 'narrow'), may hold values from -6 to 6
- kva_weight: bfloat16 [2048, 576], P('wide'), may hold values from -0.125 to 0.125
- kv_gain: bfloat16 [512], replicated, may hold values from 0.5 to 1.5
- kvb_weight: bfloat16 [512, 4096], P(None, 'narrow'), may hold values from -0.25 to 0.25
- o_weight: bfloat16 [2048, 2048], P('narrow'), may hold values from -0.125 to 0.125
- adapter_down: bfloat16 [2048, 1024], P(None, 'narrow'), may hold values from -0.125 to 0.125
- adapter_up_weight: bfloat16 [1024, 3072], P(None, 'narrow'), may hold values from -1.5 to 1.5
- lengths: int32 [64, 4], P('wide'), may hold values from 1 to 512, 1024 in all within a row
- adapter_ids: int32 [64, 4], P('wide'), may hold values from 0 to 63
- adapter_slot: int32 [64], replicated, may hold values from 0 to 63, each once
Outputs:
- hidden: bfloat16 [65536, 2048], P('wide', 'narrow')
- latent_cache: bfloat16 [65536, 576], P('wide')
The draws below stay inside these ranges and needn't reach their ends.
Inputs may be any that keep to these rules, and one draw needn't show every extreme that they name: Each row of lengths sums to 1024, and its longest prompt is exactly 512.
All inputs are finite; a program needn't handle non-finite values.
Results may differ from the reference program's by a relative error of at most 0.0095.
The reference program's roundings to bfloat16 on the way count: a program that leaves them out, or rounds other values in their place, can miss the bound.
Values may be sent and summed in bfloat16 or wider, within the bound.
No kernel may reach another device: no remote copies, remote signals or barrier semaphores. Data moves between devices by JAX's collectives and lax.ppermute only.
A program may use at most 192 MiB of HBM per device.

```python
import math
import jax
import jax.numpy as jnp
import numpy as np
from jax import lax

D = 2048
HEADS = 16
NOPE = 128
ROPE = 64
VDIM = 128
LATENT = 512
RANK = 16
ADAPTERS = 64
PROMPT_DEV = 4
TOK_DEV = 1024
TOKENS = 65536
LMAX = 512
N_WIDE = 64
N_NARROW = 2


def draw_q_weight(key, part):
    base_key = jax.random.fold_in(key, 11)
    first_key = jax.random.fold_in(base_key, 0)
    values = jnp.clip(jax.random.normal(first_key, (D, HEADS, NOPE + ROPE), jnp.float32), -4.0, 4.0)
    values = values * float(D) ** (-0.5)
    return values.reshape(D, HEADS * (NOPE + ROPE)).astype(jnp.bfloat16)


def with_ends(entries, own_key, least, high):
    spot = [jax.random.randint(jax.random.fold_in(own_key, axis), (), 0, length) for axis, length in enumerate(entries.shape)]
    main_axis = entries.shape.index(max(entries.shape))
    next_to = spot[:main_axis] + [(spot[main_axis] + 1) % entries.shape[main_axis]] + spot[main_axis + 1:]
    return entries.at[tuple(spot)].set(least).at[tuple(next_to)].set(high)


def levels(key, shape, cuts, low, top_value):
    factor_of = 1.0
    for dim, parts in cuts:
        draws = jax.random.uniform(jax.random.fold_in(jax.random.fold_in(key, 6), dim), (parts,), jnp.float32, low / len(cuts), top_value / len(cuts))
        factor_of = factor_of * jnp.repeat(jnp.exp(draws), shape[dim] // parts).reshape((-1,) + (1,) * (len(shape) - 1 - dim))
    return factor_of


def profile(count, total, bound, slope):
    portions = [(1 << 20) // math.isqrt(standing ** slope) + 1 for standing in range(2, count + 1)]
    rest, holding = total - bound - (count - 1), [1] * (count - 1)
    while rest > 0:
        free = [i for i in range(count - 1) if holding[i] < bound]
        whole, remaining = sum([portions[i] for i in free]), rest
        for i in free:
            extra = min(bound - holding[i], max(1, remaining * portions[i] // whole), rest)
            holding[i] = holding[i] + extra
            rest = rest - extra
    return np.array([bound] + holding)


def ragged_sizes(own_key, amount, total, bound, skew):
    if amount == 2:
        one = jax.random.randint(own_key, (), max(1, total - bound), min(bound, total - 1) + 1)
        return jnp.stack([one, total - one])
    tallies = jnp.asarray(profile(amount, total, bound, skew), jnp.int32)
    pairs = (amount - 1) // 2
    giver, taker = tallies[1:1 + 2 * pairs:2], tallies[2:2 + 2 * pairs:2]
    slack = jnp.minimum(giver - 1, bound - taker)
    passed = jax.random.randint(jax.random.fold_in(own_key, 1), (pairs,), 0, 1 << 20) % (slack + 1)
    tallies = tallies.at[1:1 + 2 * pairs:2].set(giver - passed).at[2:2 + 2 * pairs:2].set(taker + passed)
    return tallies[jax.random.permutation(jax.random.fold_in(own_key, 2), amount)]


def normal_values(own_key, dims, deviation, bound, pieces=(), kind=jnp.bfloat16):
    result = deviation * jax.random.normal(own_key, dims, jnp.float32)
    if pieces:
        result = result * levels(own_key, dims, pieces, -0.22, 0.18)
    return jnp.clip(result, -bound, bound).astype(kind)


def setup_inputs(seed: int = 0) -> dict:
    seeds = jax.random.split(jax.random.key(seed), 13)
    tokens = normal_values(seeds[0], (TOKENS, D), 1.0, 6.0, ((0, 64), (1, 2)))
    attn_gain = jnp.clip(1.0 + 0.1 * jax.random.normal(seeds[1], (D,), jnp.float32), 0.5, 1.5).astype(jnp.bfloat16)
    q_weight = draw_q_weight(jax.random.fold_in(seeds[12], 71), 0)
    kva_weight = normal_values(seeds[3], (D, LATENT + ROPE), D ** -0.5, 0.125, ((0, 64),))
    kv_gain = jnp.clip(1.0 + 0.1 * jax.random.normal(seeds[4], (LATENT,), jnp.float32), 0.5, 1.5).astype(jnp.bfloat16)
    kvb_weight = normal_values(seeds[5], (LATENT, HEADS * (NOPE + VDIM)), LATENT ** -0.5, 0.25, ((1, 2),))
    o_weight = normal_values(seeds[6], (HEADS * VDIM, D), (HEADS * VDIM) ** -0.5, 0.125, ((0, 2),))
    adapter_down = normal_values(seeds[7], (D, ADAPTERS * RANK), D ** -0.5, 0.125, ((1, 2),))
    adapter_up_weight = normal_values(seeds[8], (ADAPTERS * RANK, HEADS * (NOPE + ROPE)), RANK ** -0.5, 1.5, ((1, 2),))
    lengths = jax.vmap(lambda own: ragged_sizes(own, PROMPT_DEV, TOK_DEV, LMAX, 2))(jax.random.split(seeds[9], N_WIDE)).reshape((N_WIDE, PROMPT_DEV)).astype(jnp.int32)
    adapter_ids = with_ends(jax.random.randint(seeds[10], (N_WIDE, PROMPT_DEV), 0, ADAPTERS), jax.random.fold_in(seeds[10], 1), 0, ADAPTERS - 1).astype(jnp.int32)
    adapter_slot = jax.random.permutation(seeds[11], ADAPTERS).astype(jnp.int32)
    return {"tokens": tokens, "attn_gain": attn_gain, "q_weight": q_weight, "kva_weight": kva_weight, "kv_gain": kv_gain, "kvb_weight": kvb_weight, "o_weight": o_weight, "adapter_down": adapter_down, "adapter_up_weight": adapter_up_weight, "lengths": lengths, "adapter_ids": adapter_ids, "adapter_slot": adapter_slot}


EPS = 1e-06
THETA = 50000.0
ADAPTER_SCALE = 2.0

def rms_scale(values, gain):
    mean_sq = lax.optimization_barrier(jnp.mean(values * values, axis=-1, keepdims=True))
    return values * lax.rsqrt(mean_sq + EPS) * gain.astype(jnp.float32)

def rotate(values, positions):
    half = values.shape[-1] // 2
    freqs = jnp.exp(-jnp.log(THETA) * 2.0 * jnp.arange(half).astype(jnp.float32) / (2 * half))
    angle = positions.astype(jnp.float32)[:, None] * freqs[None, :]
    cosine = jnp.cos(angle)
    sine = jnp.sin(angle)
    if values.ndim == 3:
        cosine = cosine[:, None, :]
        sine = sine[:, None, :]
    first = values[..., :half]
    second = values[..., half:]
    return jnp.concatenate([first * cosine - second * sine, first * sine + second * cosine], axis=-1)

def token_tables(length_row, id_row, adapter_slot, local_pos):
    ends = jnp.cumsum(length_row).astype(jnp.int32)
    starts = (ends - length_row).astype(jnp.int32)
    prompt = lax.optimization_barrier(jnp.sum((ends[None, :] <= local_pos[:, None]).astype(jnp.int32), axis=1)).astype(jnp.int32)
    onehot = (prompt[:, None] == jnp.arange(length_row.shape[0]).astype(jnp.int32)[None, :]).astype(jnp.int32)
    position = (local_pos - lax.optimization_barrier(jnp.sum(onehot * starts[None, :], axis=1))).astype(jnp.int32)
    adapter = lax.optimization_barrier(jnp.sum(onehot * id_row[None, :], axis=1)).astype(jnp.int32)
    slot_hot = (adapter[:, None] == jnp.arange(adapter_slot.shape[0]).astype(jnp.int32)[None, :]).astype(jnp.int32)
    slot = lax.optimization_barrier(jnp.sum(slot_hot * adapter_slot[None, :], axis=1)).astype(jnp.int32)
    return (prompt, position, adapter, slot)

def reference(tokens, attn_gain, q_weight, kva_weight, kv_gain, kvb_weight, o_weight, adapter_down, adapter_up_weight, lengths, adapter_ids, adapter_slot):
    total = tokens.shape[0]
    block = total // N_WIDE
    local_pos = jnp.arange(block).astype(jnp.int32)
    tables = jax.vmap(lambda lr, ir: token_tables(lr, ir, adapter_slot, local_pos))(lengths, adapter_ids)
    prompt, position, adapter, slot = [v.reshape(total).astype(jnp.int32) for v in tables]
    normed = rms_scale(tokens.astype(jnp.float32), attn_gain).astype(jnp.bfloat16)
    query_vectors = jnp.dot(normed, q_weight, preferred_element_type=jnp.float32)
    low = jnp.dot(normed, adapter_down, preferred_element_type=jnp.float32).reshape(total, ADAPTERS, RANK)
    pick = (slot[:, None] == jnp.arange(ADAPTERS).astype(jnp.int32)[None, :]).astype(jnp.float32)
    lowrank = lax.optimization_barrier(jnp.sum(low * pick[:, :, None], axis=1)).astype(jnp.bfloat16)
    usage = (adapter[:, None] == jnp.arange(ADAPTERS).astype(jnp.int32)[None, :]).astype(jnp.bfloat16)
    spread_rows = (usage[:, :, None] * lowrank[:, None, :]).reshape(total, ADAPTERS * RANK)
    query_vectors = query_vectors + ADAPTER_SCALE * jnp.dot(spread_rows, adapter_up_weight, preferred_element_type=jnp.float32)
    query_vectors = query_vectors.reshape(total, HEADS, NOPE + ROPE)
    query_vectors = jnp.concatenate([query_vectors[..., :NOPE], rotate(query_vectors[..., NOPE:], position)], axis=-1).astype(jnp.bfloat16)
    kv_pre = jnp.dot(normed, kva_weight, preferred_element_type=jnp.float32)
    latent = rms_scale(kv_pre[:, :LATENT], kv_gain).astype(jnp.bfloat16)
    key_rope = rotate(kv_pre[:, LATENT:], position).astype(jnp.bfloat16)
    latent_cache = jnp.concatenate([latent, key_rope], axis=1)
    expanded = jnp.dot(latent, kvb_weight, preferred_element_type=jnp.float32).astype(jnp.bfloat16)
    expanded = expanded.reshape(total, HEADS, NOPE + VDIM)
    scale = 1.0 / jnp.sqrt(jnp.float32(NOPE + ROPE))

    def attend(index):
        first = (index * block).astype(jnp.int32)
        query_block = lax.dynamic_slice_in_dim(query_vectors, first, block, 0).astype(jnp.float32)
        ex = lax.dynamic_slice_in_dim(expanded, first, block, 0).astype(jnp.float32)
        kr = lax.dynamic_slice_in_dim(key_rope, first, block, 0).astype(jnp.float32)
        pr = lax.dynamic_slice_in_dim(prompt, first, block, 0)
        scores = jnp.einsum('qhd,khd->hqk', query_block[..., :NOPE], ex[..., :NOPE])
        scores = (scores + jnp.einsum('qhd,kd->hqk', query_block[..., NOPE:], kr)) * scale
        allowed = (pr[None, :] == pr[:, None]) & (local_pos[None, :] <= local_pos[:, None])
        scores = jnp.where(allowed[None, :, :], scores, jnp.float32(-1e+30))
        top = lax.optimization_barrier(jnp.max(scores, axis=-1, keepdims=True))
        expo = jnp.exp(scores - top)
        weights = (expo / lax.optimization_barrier(jnp.sum(expo, axis=-1, keepdims=True))).astype(jnp.bfloat16)
        out = jnp.einsum('hqk,khd->qhd', weights.astype(jnp.float32), ex[..., NOPE:]).astype(jnp.bfloat16)
        return out.reshape(block, HEADS * VDIM)
    attended = lax.map(attend, jnp.arange(N_WIDE).astype(jnp.int32)).reshape(total, HEADS * VDIM)
    group = HEADS * VDIM // N_NARROW
    projected = jnp.zeros((total, D), jnp.float32)
    for index in range(N_NARROW):
        part = jnp.dot(attended[:, index * group:(index + 1) * group], o_weight[index * group:(index + 1) * group, :], preferred_element_type=jnp.float32)
        part = lax.optimization_barrier(part.astype(jnp.bfloat16))
        projected = projected + part.astype(jnp.float32)
    hidden = (tokens.astype(jnp.float32) + projected).astype(jnp.bfloat16)
    return (hidden, latent_cache)
```

```python
import jax
import jax.numpy as jnp
from jax import lax
from jax.sharding import PartitionSpec as P

NOPE = 128
ROPE = 64
VDIM = 128
LATENT = 512
RANK = 16


EPS = 1e-06
THETA = 50000.0
ADAPTER_SCALE = 2.0


def rms_scale(values, gain):
    mean_sq = jnp.mean(values * values, axis=-1, keepdims=True)
    return values * lax.rsqrt(mean_sq + EPS) * gain.astype(jnp.float32)


def rotate(values, positions):
    half = values.shape[-1] // 2
    freqs = jnp.exp(-jnp.log(THETA) * 2.0 * jnp.arange(half).astype(jnp.float32) / (2 * half))
    angle = positions.astype(jnp.float32)[:, None] * freqs[None, :]
    cosine = jnp.cos(angle)
    sine = jnp.sin(angle)
    if values.ndim == 3:
        cosine = cosine[:, None, :]
        sine = sine[:, None, :]
    first = values[..., :half]
    second = values[..., half:]
    return jnp.concatenate(
        [first * cosine - second * sine, first * sine + second * cosine], axis=-1
    )


def token_tables(length_row, id_row, adapter_slot, local_pos):
    ends = jnp.cumsum(length_row)
    starts = ends - length_row
    prompt = jnp.sum((ends[None, :] <= local_pos[:, None]).astype(jnp.int32), axis=1)
    onehot = (prompt[:, None] == jnp.arange(length_row.shape[0])[None, :]).astype(jnp.int32)
    position = local_pos - jnp.sum(onehot * starts[None, :], axis=1)
    adapter = jnp.sum(onehot * id_row[None, :], axis=1)
    slot_hot = (adapter[:, None] == jnp.arange(adapter_slot.shape[0])[None, :]).astype(jnp.int32)
    slot = jnp.sum(slot_hot * adapter_slot[None, :], axis=1)
    return (prompt, position, adapter, slot)


def swap(values):
    return lax.ppermute(values, "narrow", perm=[(0, 1), (1, 0)])


def body(
    tokens,
    attn_gain,
    q_weight,
    kva_weight,
    kv_gain,
    kvb_weight,
    o_weight,
    adapter_down,
    adapter_up_weight,
    lengths,
    adapter_ids,
    adapter_slot,
):
    rows = tokens.shape[0]
    half_width = tokens.shape[1]
    heads_here = o_weight.shape[0] // VDIM
    prompts_here = lengths.shape[1]
    q_cols = q_weight.shape[1]
    me = lax.axis_index("narrow")
    mine_first = me == 0

    joined = jnp.concatenate([q_weight, kva_weight], axis=1)
    joined = lax.all_gather(joined, "wide", axis=0, tiled=True)

    other = swap(tokens)
    whole = jnp.concatenate(
        [jnp.where(mine_first, tokens, other), jnp.where(mine_first, other, tokens)], axis=1
    )

    slots_here = adapter_down.shape[1] // RANK
    prompt_ids = adapter_ids[0]
    id_hot = (prompt_ids[:, None] == jnp.arange(adapter_slot.shape[0])[None, :]).astype(jnp.int32)
    prompt_slot = jnp.sum(id_hot * adapter_slot[None, :], axis=1)
    owner = prompt_slot // slots_here
    local_slot = prompt_slot % slots_here
    picked = jnp.concatenate(
        [
            lax.dynamic_slice_in_dim(adapter_down, local_slot[p] * RANK, RANK, 1)
            for p in range(prompts_here)
        ],
        axis=1,
    )
    picked_other = swap(picked)
    own_block = jnp.repeat(owner == me, RANK)
    chosen = jnp.where(own_block[None, :], picked, picked_other)

    normed = rms_scale(whole.astype(jnp.float32), attn_gain).astype(jnp.bfloat16)
    local_pos = jnp.arange(rows)
    prompt, position, adapter, slot = token_tables(
        lengths[0], adapter_ids[0], adapter_slot, local_pos
    )
    projections = jnp.dot(normed, joined, preferred_element_type=jnp.float32)
    query_vectors = projections[:, :q_cols]
    kv_pre = projections[:, q_cols:]
    member = (prompt[:, None] == jnp.arange(prompts_here)[None, :]).astype(jnp.float32)
    low = jnp.dot(normed, chosen, preferred_element_type=jnp.float32).reshape(
        rows, prompts_here, RANK
    )
    lowrank = jnp.sum(low * member[:, :, None], axis=1).astype(jnp.bfloat16)
    up_blocks = [
        lax.dynamic_slice_in_dim(adapter_up_weight, prompt_ids[prompt_index] * RANK, RANK, 0)
        for prompt_index in range(prompts_here)
    ]
    up_weight_rows = jnp.concatenate(up_blocks, axis=0)
    spread_rows = (member.astype(jnp.bfloat16)[:, :, None] * lowrank[:, None, :]).reshape(
        rows, prompts_here * RANK
    )
    query_vectors = query_vectors + ADAPTER_SCALE * jnp.dot(
        spread_rows, up_weight_rows, preferred_element_type=jnp.float32
    )
    query_vectors = query_vectors.reshape(rows, heads_here, NOPE + ROPE)
    query_vectors = jnp.concatenate(
        [query_vectors[..., :NOPE], rotate(query_vectors[..., NOPE:], position)], axis=-1
    ).astype(jnp.bfloat16)
    latent = rms_scale(kv_pre[:, :LATENT], kv_gain).astype(jnp.bfloat16)
    key_rope = rotate(kv_pre[:, LATENT:], position).astype(jnp.bfloat16)
    latent_cache = jnp.concatenate([latent, key_rope], axis=1)
    expanded = jnp.dot(latent, kvb_weight, preferred_element_type=jnp.float32).astype(jnp.bfloat16)
    expanded = expanded.reshape(rows, heads_here, NOPE + VDIM)
    key_nope = expanded[..., :NOPE]
    values = expanded[..., NOPE:]
    scale = 1.0 / jnp.sqrt(jnp.float32(NOPE + ROPE))
    scores = jnp.einsum(
        "qhd,khd->hqk", query_vectors[..., :NOPE], key_nope, preferred_element_type=jnp.float32
    )
    scores = scores + jnp.einsum(
        "qhd,kd->hqk", query_vectors[..., NOPE:], key_rope, preferred_element_type=jnp.float32
    )
    scores = scores * scale
    allowed = (prompt[None, :] == prompt[:, None]) & (local_pos[None, :] <= local_pos[:, None])
    scores = jnp.where(allowed[None, :, :], scores, jnp.float32(-1e30))
    top = jnp.max(scores, axis=-1, keepdims=True)
    expo = jnp.exp(scores - top)
    weights = (expo / jnp.sum(expo, axis=-1, keepdims=True)).astype(jnp.bfloat16)
    attended = jnp.einsum(
        "hqk,khd->qhd", weights, values, preferred_element_type=jnp.float32
    ).astype(jnp.bfloat16)
    attended = attended.reshape(rows, heads_here * VDIM)
    their_cols = lax.dynamic_slice_in_dim(o_weight, (1 - me) * half_width, half_width, 1)
    my_cols = lax.dynamic_slice_in_dim(o_weight, me * half_width, half_width, 1)
    theirs = jnp.dot(attended, their_cols, preferred_element_type=jnp.float32).astype(jnp.bfloat16)
    received = swap(theirs)
    mine = jnp.dot(attended, my_cols, preferred_element_type=jnp.float32).astype(jnp.bfloat16)
    projected = mine.astype(jnp.float32) + received.astype(jnp.float32)
    hidden = (tokens.astype(jnp.float32) + projected).astype(jnp.bfloat16)
    return (hidden, latent_cache)


def solution(mesh):
    return jax.shard_map(
        body,
        mesh=mesh,
        in_specs=(
            P("wide", "narrow"),
            P(),
            P("wide", "narrow"),
            P("wide", None),
            P(),
            P(None, "narrow"),
            P("narrow", None),
            P(None, "narrow"),
            P(None, "narrow"),
            P("wide", None),
            P("wide", None),
            P(),
        ),
        out_specs=(P("wide", "narrow"), P("wide", None)),
        check_vma=False,
    )
```

```python
import jax
import jax.numpy as jnp
from jax import lax
from jax.sharding import PartitionSpec as P
from jax.experimental import pallas as pl
from jax.experimental.pallas import tpu as pltpu

NOPE = 128
ROPE = 64
VDIM = 128
LATENT = 512
RANK = 16
BLOCK = 128


EPS = 1e-06
THETA = 50000.0
ADAPTER_SCALE = 2.0


def rms_scale(values, gain):
    mean_sq = jnp.mean(values * values, axis=-1, keepdims=True)
    return values * lax.rsqrt(mean_sq + EPS) * gain.astype(jnp.float32)


def rotate(values, positions):
    half = values.shape[-1] // 2
    freqs = jnp.exp(-jnp.log(THETA) * 2.0 * jnp.arange(half).astype(jnp.float32) / (2 * half))
    angle = positions.astype(jnp.float32)[:, None] * freqs[None, :]
    cosine = jnp.cos(angle)
    sine = jnp.sin(angle)
    if values.ndim == 3:
        cosine = cosine[:, None, :]
        sine = sine[:, None, :]
    first = values[..., :half]
    second = values[..., half:]
    return jnp.concatenate(
        [first * cosine - second * sine, first * sine + second * cosine], axis=-1
    )


def token_tables(length_row, id_row, adapter_slot, local_pos):
    ends = jnp.cumsum(length_row)
    starts = ends - length_row
    prompt = jnp.sum((ends[None, :] <= local_pos[:, None]).astype(jnp.int32), axis=1)
    onehot = (prompt[:, None] == jnp.arange(length_row.shape[0])[None, :]).astype(jnp.int32)
    position = local_pos - jnp.sum(onehot * starts[None, :], axis=1)
    adapter = jnp.sum(onehot * id_row[None, :], axis=1)
    slot_hot = (adapter[:, None] == jnp.arange(adapter_slot.shape[0])[None, :]).astype(jnp.int32)
    slot = jnp.sum(slot_hot * adapter_slot[None, :], axis=1)
    return (prompt, position, adapter, slot)


def attention_kernel(first_ref, q_nope_ref, q_rope_ref, kv_ref, kr_ref, kst_ref, o_ref, s_buf):
    i = pl.program_id(0)
    heads = q_rope_ref.shape[0]
    scale = 1.0 / jnp.sqrt(jnp.float32(NOPE + ROPE))
    lo = first_ref[i]
    row = i * BLOCK + lax.broadcasted_iota(jnp.int32, (BLOCK, BLOCK), 0)
    kst = kst_ref[...]
    for h in range(heads):
        qn = q_nope_ref[:, h * NOPE:(h + 1) * NOPE]
        qr = q_rope_ref[h]

        def score_step(c, top):
            start = pl.multiple_of(c * BLOCK, BLOCK)
            kn = kv_ref[pl.ds(start, BLOCK), h * (NOPE + VDIM):h * (NOPE + VDIM) + NOPE]
            kr = kr_ref[pl.ds(start, BLOCK), :]
            s = lax.dot_general(qn, kn, (((1,), (1,)), ((), ())), preferred_element_type=jnp.float32)
            s = s + lax.dot_general(qr, kr, (((1,), (1,)), ((), ())), preferred_element_type=jnp.float32)
            s = s * scale
            col = start + lax.broadcasted_iota(jnp.int32, (BLOCK, BLOCK), 1)
            allowed = (col >= kst) & (col <= row)
            s = jnp.where(allowed, s, jnp.float32(-1e30))
            s_buf[c] = s
            return jnp.maximum(top, jnp.max(s, axis=1, keepdims=True))

        top = lax.fori_loop(lo, i + 1, score_step, jnp.full((BLOCK, 1), -jnp.inf, jnp.float32))

        def exp_step(c, total):
            e = jnp.exp(s_buf[c] - top)
            s_buf[c] = e
            return total + jnp.sum(e, axis=1, keepdims=True)

        total = lax.fori_loop(lo, i + 1, exp_step, jnp.zeros((BLOCK, 1), jnp.float32))

        def pv_step(c, acc):
            start = pl.multiple_of(c * BLOCK, BLOCK)
            w = (s_buf[c] / total).astype(jnp.bfloat16)
            v = kv_ref[pl.ds(start, BLOCK), h * (NOPE + VDIM) + NOPE:(h + 1) * (NOPE + VDIM)]
            return acc + jnp.dot(w, v, preferred_element_type=jnp.float32)

        acc = lax.fori_loop(lo, i + 1, pv_step, jnp.zeros((BLOCK, VDIM), jnp.float32))
        o_ref[:, h * VDIM:(h + 1) * VDIM] = acc.astype(o_ref.dtype)


def attend(q_nope, q_rope, kv, key_rope, key_start):
    rows = q_nope.shape[0]
    heads = q_rope.shape[0]
    blocks = rows // BLOCK
    first = key_start[::BLOCK] // BLOCK
    grid_spec = pltpu.PrefetchScalarGridSpec(
        num_scalar_prefetch=1,
        grid=(blocks,),
        in_specs=[
            pl.BlockSpec((BLOCK, heads * NOPE), lambda i, f: (i, 0)),
            pl.BlockSpec((heads, BLOCK, ROPE), lambda i, f: (0, i, 0)),
            pl.BlockSpec((rows, heads * (NOPE + VDIM)), lambda i, f: (0, 0)),
            pl.BlockSpec((rows, ROPE), lambda i, f: (0, 0)),
            pl.BlockSpec((BLOCK, 1), lambda i, f: (i, 0)),
        ],
        out_specs=pl.BlockSpec((BLOCK, heads * VDIM), lambda i, f: (i, 0)),
        scratch_shapes=[pltpu.VMEM((blocks, BLOCK, BLOCK), jnp.float32)],
    )
    return pl.pallas_call(
        attention_kernel,
        grid_spec=grid_spec,
        out_shape=jax.ShapeDtypeStruct((rows, heads * VDIM), jnp.bfloat16),
    )(first, q_nope, q_rope, kv, key_rope, key_start[:, None])


def swap(values):
    return lax.ppermute(values, "narrow", perm=[(0, 1), (1, 0)])


def body(
    tokens,
    attn_gain,
    q_weight,
    kva_weight,
    kv_gain,
    kvb_weight,
    o_weight,
    adapter_down,
    adapter_up_weight,
    lengths,
    adapter_ids,
    adapter_slot,
):
    rows = tokens.shape[0]
    half_width = tokens.shape[1]
    heads_here = o_weight.shape[0] // VDIM
    prompts_here = lengths.shape[1]
    q_cols = q_weight.shape[1]
    me = lax.axis_index("narrow")
    mine_first = me == 0

    joined = jnp.concatenate([q_weight, kva_weight], axis=1)
    joined = lax.all_gather(joined, "wide", axis=0, tiled=True)

    other = swap(tokens)
    whole = jnp.concatenate(
        [jnp.where(mine_first, tokens, other), jnp.where(mine_first, other, tokens)], axis=1
    )

    slots_here = adapter_down.shape[1] // RANK
    prompt_ids = adapter_ids[0]
    id_hot = (prompt_ids[:, None] == jnp.arange(adapter_slot.shape[0])[None, :]).astype(jnp.int32)
    prompt_slot = jnp.sum(id_hot * adapter_slot[None, :], axis=1)
    owner = prompt_slot // slots_here
    local_slot = prompt_slot % slots_here
    picked = jnp.concatenate(
        [
            lax.dynamic_slice_in_dim(adapter_down, local_slot[p] * RANK, RANK, 1)
            for p in range(prompts_here)
        ],
        axis=1,
    )
    picked_other = swap(picked)
    own_block = jnp.repeat(owner == me, RANK)
    chosen = jnp.where(own_block[None, :], picked, picked_other)

    normed = rms_scale(whole.astype(jnp.float32), attn_gain).astype(jnp.bfloat16)
    local_pos = jnp.arange(rows)
    prompt, position, adapter, slot = token_tables(
        lengths[0], adapter_ids[0], adapter_slot, local_pos
    )
    projections = jnp.dot(normed, joined, preferred_element_type=jnp.float32)
    query_vectors = projections[:, :q_cols]
    kv_pre = projections[:, q_cols:]
    member = (prompt[:, None] == jnp.arange(prompts_here)[None, :]).astype(jnp.float32)
    low = jnp.dot(normed, chosen, preferred_element_type=jnp.float32).reshape(
        rows, prompts_here, RANK
    )
    lowrank = jnp.sum(low * member[:, :, None], axis=1).astype(jnp.bfloat16)
    up_blocks = [
        lax.dynamic_slice_in_dim(adapter_up_weight, prompt_ids[prompt_index] * RANK, RANK, 0)
        for prompt_index in range(prompts_here)
    ]
    up_weight_rows = jnp.concatenate(up_blocks, axis=0)
    spread_rows = (member.astype(jnp.bfloat16)[:, :, None] * lowrank[:, None, :]).reshape(
        rows, prompts_here * RANK
    )
    query_vectors = query_vectors + ADAPTER_SCALE * jnp.dot(
        spread_rows, up_weight_rows, preferred_element_type=jnp.float32
    )
    query_vectors = query_vectors.reshape(rows, heads_here, NOPE + ROPE)
    q_nope = query_vectors[..., :NOPE].astype(jnp.bfloat16).reshape(rows, heads_here * NOPE)
    q_rope = jnp.transpose(
        rotate(query_vectors[..., NOPE:], position).astype(jnp.bfloat16), (1, 0, 2)
    )
    latent = rms_scale(kv_pre[:, :LATENT], kv_gain).astype(jnp.bfloat16)
    key_rope = rotate(kv_pre[:, LATENT:], position).astype(jnp.bfloat16)
    latent_cache = jnp.concatenate([latent, key_rope], axis=1)
    expanded = jnp.dot(latent, kvb_weight, preferred_element_type=jnp.float32).astype(jnp.bfloat16)
    key_start = (local_pos - position).astype(jnp.int32)
    attended = attend(q_nope, q_rope, expanded, key_rope, key_start)
    their_cols = lax.dynamic_slice_in_dim(o_weight, (1 - me) * half_width, half_width, 1)
    my_cols = lax.dynamic_slice_in_dim(o_weight, me * half_width, half_width, 1)
    theirs = jnp.dot(attended, their_cols, preferred_element_type=jnp.float32).astype(jnp.bfloat16)
    received = swap(theirs)
    mine = jnp.dot(attended, my_cols, preferred_element_type=jnp.float32).astype(jnp.bfloat16)
    projected = mine.astype(jnp.float32) + received.astype(jnp.float32)
    hidden = (tokens.astype(jnp.float32) + projected).astype(jnp.bfloat16)
    return (hidden, latent_cache)


def solution(mesh):
    return jax.shard_map(
        body,
        mesh=mesh,
        in_specs=(
            P("wide", "narrow"),
            P(),
            P("wide", "narrow"),
            P("wide", None),
            P(),
            P(None, "narrow"),
            P("narrow", None),
            P(None, "narrow"),
            P(None, "narrow"),
            P("wide", None),
            P("wide", None),
            P(),
        ),
        out_specs=(P("wide", "narrow"), P("wide", None)),
        check_vma=False,
    )
```

```python
import jax
import jax.numpy as jnp
from jax import lax
from jax.sharding import PartitionSpec as P
from jax.experimental import pallas as pl
from jax.experimental.pallas import tpu as pltpu

NOPE = 128
ROPE = 64
VDIM = 128
LATENT = 512
RANK = 16
LMAX = 512
QBLOCK = 256
WINDOW = QBLOCK + LMAX


EPS = 1e-06
THETA = 50000.0
ADAPTER_SCALE = 2.0


def rms_scale(values, gain):
    mean_sq = jnp.mean(values * values, axis=-1, keepdims=True)
    return values * lax.rsqrt(mean_sq + EPS) * gain.astype(jnp.float32)


def rotate(values, positions):
    half = values.shape[-1] // 2
    freqs = jnp.exp(-jnp.log(THETA) * 2.0 * jnp.arange(half).astype(jnp.float32) / (2 * half))
    angle = positions.astype(jnp.float32)[:, None] * freqs[None, :]
    cosine = jnp.cos(angle)
    sine = jnp.sin(angle)
    if values.ndim == 3:
        cosine = cosine[:, None, :]
        sine = sine[:, None, :]
    first = values[..., :half]
    second = values[..., half:]
    return jnp.concatenate(
        [first * cosine - second * sine, first * sine + second * cosine], axis=-1
    )


def token_tables(length_row, id_row, adapter_slot, local_pos):
    ends = jnp.cumsum(length_row)
    starts = ends - length_row
    prompt = jnp.sum((ends[None, :] <= local_pos[:, None]).astype(jnp.int32), axis=1)
    onehot = (prompt[:, None] == jnp.arange(length_row.shape[0])[None, :]).astype(jnp.int32)
    position = local_pos - jnp.sum(onehot * starts[None, :], axis=1)
    adapter = jnp.sum(onehot * id_row[None, :], axis=1)
    slot_hot = (adapter[:, None] == jnp.arange(adapter_slot.shape[0])[None, :]).astype(jnp.int32)
    slot = jnp.sum(slot_hot * adapter_slot[None, :], axis=1)
    return (prompt, position, adapter, slot)


def attention_kernel(q_nope_ref, q_rope_ref, kv_ref, kr_ref, kst_ref, o_ref):
    i = pl.program_id(0)
    heads = q_rope_ref.shape[0]
    scale = 1.0 / jnp.sqrt(jnp.float32(NOPE + ROPE))
    start = pl.multiple_of(jnp.maximum(i * QBLOCK - LMAX, 0), 128)
    row = i * QBLOCK + lax.broadcasted_iota(jnp.int32, (QBLOCK, WINDOW), 0)
    col = start + lax.broadcasted_iota(jnp.int32, (QBLOCK, WINDOW), 1)
    allowed = (col >= kst_ref[...]) & (col <= row)
    kr = kr_ref[pl.ds(start, WINDOW), :]
    for h in range(heads):
        qn = q_nope_ref[:, h * NOPE:(h + 1) * NOPE]
        qr = q_rope_ref[h]
        kn = kv_ref[pl.ds(start, WINDOW), h * (NOPE + VDIM):h * (NOPE + VDIM) + NOPE]
        s = lax.dot_general(qn, kn, (((1,), (1,)), ((), ())), preferred_element_type=jnp.float32)
        s = s + lax.dot_general(qr, kr, (((1,), (1,)), ((), ())), preferred_element_type=jnp.float32)
        s = jnp.where(allowed, s * scale, jnp.float32(-1e30))
        top = jnp.max(s, axis=1, keepdims=True)
        e = jnp.exp(s - top)
        w = (e / jnp.sum(e, axis=1, keepdims=True)).astype(jnp.bfloat16)
        v = kv_ref[pl.ds(start, WINDOW), h * (NOPE + VDIM) + NOPE:(h + 1) * (NOPE + VDIM)]
        o_ref[:, h * VDIM:(h + 1) * VDIM] = jnp.dot(
            w, v, preferred_element_type=jnp.float32
        ).astype(o_ref.dtype)


def attend(q_nope, q_rope, kv, key_rope, key_start):
    rows = q_nope.shape[0]
    heads = q_rope.shape[0]
    return pl.pallas_call(
        attention_kernel,
        grid=(rows // QBLOCK,),
        in_specs=[
            pl.BlockSpec((QBLOCK, heads * NOPE), lambda i: (i, 0)),
            pl.BlockSpec((heads, QBLOCK, ROPE), lambda i: (0, i, 0)),
            pl.BlockSpec((rows, heads * (NOPE + VDIM)), lambda i: (0, 0)),
            pl.BlockSpec((rows, ROPE), lambda i: (0, 0)),
            pl.BlockSpec((QBLOCK, 1), lambda i: (i, 0)),
        ],
        out_specs=pl.BlockSpec((QBLOCK, heads * VDIM), lambda i: (i, 0)),
        out_shape=jax.ShapeDtypeStruct((rows, heads * VDIM), jnp.bfloat16),
    )(q_nope, q_rope, kv, key_rope, key_start[:, None])


def swap(values):
    return lax.ppermute(values, "narrow", perm=[(0, 1), (1, 0)])


def body(
    tokens,
    attn_gain,
    q_weight,
    kva_weight,
    kv_gain,
    kvb_weight,
    o_weight,
    adapter_down,
    adapter_up_weight,
    lengths,
    adapter_ids,
    adapter_slot,
):
    rows = tokens.shape[0]
    half_width = tokens.shape[1]
    heads_here = o_weight.shape[0] // VDIM
    prompts_here = lengths.shape[1]
    q_cols = q_weight.shape[1]
    me = lax.axis_index("narrow")
    mine_first = me == 0

    joined = jnp.concatenate([q_weight, kva_weight], axis=1)
    joined = lax.all_gather(joined, "wide", axis=0, tiled=True)

    other = swap(tokens)
    whole = jnp.concatenate(
        [jnp.where(mine_first, tokens, other), jnp.where(mine_first, other, tokens)], axis=1
    )

    slots_here = adapter_down.shape[1] // RANK
    prompt_ids = adapter_ids[0]
    id_hot = (prompt_ids[:, None] == jnp.arange(adapter_slot.shape[0])[None, :]).astype(jnp.int32)
    prompt_slot = jnp.sum(id_hot * adapter_slot[None, :], axis=1)
    owner = prompt_slot // slots_here
    local_slot = prompt_slot % slots_here
    picked = jnp.concatenate(
        [
            lax.dynamic_slice_in_dim(adapter_down, local_slot[p] * RANK, RANK, 1)
            for p in range(prompts_here)
        ],
        axis=1,
    )
    picked_other = swap(picked)
    own_block = jnp.repeat(owner == me, RANK)
    chosen = jnp.where(own_block[None, :], picked, picked_other)

    normed = rms_scale(whole.astype(jnp.float32), attn_gain).astype(jnp.bfloat16)
    local_pos = jnp.arange(rows)
    prompt, position, adapter, slot = token_tables(
        lengths[0], adapter_ids[0], adapter_slot, local_pos
    )
    projections = jnp.dot(normed, joined, preferred_element_type=jnp.float32)
    query_vectors = projections[:, :q_cols]
    kv_pre = projections[:, q_cols:]
    member = (prompt[:, None] == jnp.arange(prompts_here)[None, :]).astype(jnp.float32)
    low = jnp.dot(normed, chosen, preferred_element_type=jnp.float32).reshape(
        rows, prompts_here, RANK
    )
    lowrank = jnp.sum(low * member[:, :, None], axis=1).astype(jnp.bfloat16)
    up_blocks = [
        lax.dynamic_slice_in_dim(adapter_up_weight, prompt_ids[prompt_index] * RANK, RANK, 0)
        for prompt_index in range(prompts_here)
    ]
    up_weight_rows = jnp.concatenate(up_blocks, axis=0)
    spread_rows = (member.astype(jnp.bfloat16)[:, :, None] * lowrank[:, None, :]).reshape(
        rows, prompts_here * RANK
    )
    query_vectors = query_vectors + ADAPTER_SCALE * jnp.dot(
        spread_rows, up_weight_rows, preferred_element_type=jnp.float32
    )
    query_vectors = query_vectors.reshape(rows, heads_here, NOPE + ROPE)
    q_nope = query_vectors[..., :NOPE].astype(jnp.bfloat16).reshape(rows, heads_here * NOPE)
    q_rope = jnp.transpose(
        rotate(query_vectors[..., NOPE:], position).astype(jnp.bfloat16), (1, 0, 2)
    )
    latent = rms_scale(kv_pre[:, :LATENT], kv_gain).astype(jnp.bfloat16)
    key_rope = rotate(kv_pre[:, LATENT:], position).astype(jnp.bfloat16)
    latent_cache = jnp.concatenate([latent, key_rope], axis=1)
    expanded = jnp.dot(latent, kvb_weight, preferred_element_type=jnp.float32).astype(jnp.bfloat16)
    key_start = (local_pos - position).astype(jnp.int32)
    attended = attend(q_nope, q_rope, expanded, key_rope, key_start)
    their_cols = lax.dynamic_slice_in_dim(o_weight, (1 - me) * half_width, half_width, 1)
    my_cols = lax.dynamic_slice_in_dim(o_weight, me * half_width, half_width, 1)
    theirs = jnp.dot(attended, their_cols, preferred_element_type=jnp.float32).astype(jnp.bfloat16)
    received = swap(theirs)
    mine = jnp.dot(attended, my_cols, preferred_element_type=jnp.float32).astype(jnp.bfloat16)
    projected = mine.astype(jnp.float32) + received.astype(jnp.float32)
    hidden = (tokens.astype(jnp.float32) + projected).astype(jnp.bfloat16)
    return (hidden, latent_cache)


def solution(mesh):
    return jax.shard_map(
        body,
        mesh=mesh,
        in_specs=(
            P("wide", "narrow"),
            P(),
            P("wide", "narrow"),
            P("wide", None),
            P(),
            P(None, "narrow"),
            P("narrow", None),
            P(None, "narrow"),
            P(None, "narrow"),
            P("wide", None),
            P("wide", None),
            P(),
        ),
        out_specs=(P("wide", "narrow"), P("wide", None)),
        check_vma=False,
    )
```

```python
import jax
import jax.numpy as jnp
from jax import lax
from jax.sharding import PartitionSpec as P
from jax.experimental import pallas as pl
from jax.experimental.pallas import tpu as pltpu

NOPE = 128
ROPE = 64
VDIM = 128
LATENT = 512
RANK = 16
LMAX = 512
QBLOCK = 128
WINDOW = QBLOCK + LMAX


EPS = 1e-06
THETA = 50000.0
ADAPTER_SCALE = 2.0


def rms_scale(values, gain):
    mean_sq = jnp.mean(values * values, axis=-1, keepdims=True)
    return values * lax.rsqrt(mean_sq + EPS) * gain.astype(jnp.float32)


def rotate(values, positions):
    half = values.shape[-1] // 2
    freqs = jnp.exp(-jnp.log(THETA) * 2.0 * jnp.arange(half).astype(jnp.float32) / (2 * half))
    angle = positions.astype(jnp.float32)[:, None] * freqs[None, :]
    cosine = jnp.cos(angle)
    sine = jnp.sin(angle)
    if values.ndim == 3:
        cosine = cosine[:, None, :]
        sine = sine[:, None, :]
    first = values[..., :half]
    second = values[..., half:]
    return jnp.concatenate(
        [first * cosine - second * sine, first * sine + second * cosine], axis=-1
    )


def token_tables(length_row, id_row, adapter_slot, local_pos):
    ends = jnp.cumsum(length_row)
    starts = ends - length_row
    prompt = jnp.sum((ends[None, :] <= local_pos[:, None]).astype(jnp.int32), axis=1)
    onehot = (prompt[:, None] == jnp.arange(length_row.shape[0])[None, :]).astype(jnp.int32)
    position = local_pos - jnp.sum(onehot * starts[None, :], axis=1)
    adapter = jnp.sum(onehot * id_row[None, :], axis=1)
    slot_hot = (adapter[:, None] == jnp.arange(adapter_slot.shape[0])[None, :]).astype(jnp.int32)
    slot = jnp.sum(slot_hot * adapter_slot[None, :], axis=1)
    return (prompt, position, adapter, slot)


def attention_kernel(q_nope_ref, q_rope_ref, kv_ref, kr_ref, kst_ref, o_ref):
    i = pl.program_id(0)
    heads = q_rope_ref.shape[0]
    scale = 1.0 / jnp.sqrt(jnp.float32(NOPE + ROPE))
    start = pl.multiple_of(jnp.maximum(i * QBLOCK - LMAX, 0), 128)
    row = i * QBLOCK + lax.broadcasted_iota(jnp.int32, (QBLOCK, WINDOW), 0)
    col = start + lax.broadcasted_iota(jnp.int32, (QBLOCK, WINDOW), 1)
    allowed = (col >= kst_ref[...]) & (col <= row)
    kr = kr_ref[pl.ds(start, WINDOW), :]
    for h in range(heads):
        qn = q_nope_ref[:, h * NOPE:(h + 1) * NOPE]
        qr = q_rope_ref[h]
        kn = kv_ref[pl.ds(start, WINDOW), h * (NOPE + VDIM):h * (NOPE + VDIM) + NOPE]
        s = lax.dot_general(qn, kn, (((1,), (1,)), ((), ())), preferred_element_type=jnp.float32)
        s = s + lax.dot_general(qr, kr, (((1,), (1,)), ((), ())), preferred_element_type=jnp.float32)
        s = jnp.where(allowed, s * scale, jnp.float32(-1e30))
        top = jnp.max(s, axis=1, keepdims=True)
        e = jnp.exp(s - top)
        w = (e * (1.0 / jnp.sum(e, axis=1, keepdims=True))).astype(jnp.bfloat16)
        v = kv_ref[pl.ds(start, WINDOW), h * (NOPE + VDIM) + NOPE:(h + 1) * (NOPE + VDIM)]
        o_ref[:, h * VDIM:(h + 1) * VDIM] = jnp.dot(
            w, v, preferred_element_type=jnp.float32
        ).astype(o_ref.dtype)


def attend(q_nope, q_rope, kv, key_rope, key_start):
    rows = q_nope.shape[0]
    heads = q_rope.shape[0]
    return pl.pallas_call(
        attention_kernel,
        grid=(rows // QBLOCK,),
        in_specs=[
            pl.BlockSpec((QBLOCK, heads * NOPE), lambda i: (i, 0)),
            pl.BlockSpec((heads, QBLOCK, ROPE), lambda i: (0, i, 0)),
            pl.BlockSpec((rows, heads * (NOPE + VDIM)), lambda i: (0, 0)),
            pl.BlockSpec((rows, ROPE), lambda i: (0, 0)),
            pl.BlockSpec((QBLOCK, 1), lambda i: (i, 0)),
        ],
        out_specs=pl.BlockSpec((QBLOCK, heads * VDIM), lambda i: (i, 0)),
        out_shape=jax.ShapeDtypeStruct((rows, heads * VDIM), jnp.bfloat16),
    )(q_nope, q_rope, kv, key_rope, key_start[:, None])


def split_heads(weight, heads):
    parts = weight.reshape(weight.shape[0], heads, NOPE + ROPE)
    half = ROPE // 2
    return jnp.concatenate(
        [
            parts[..., :NOPE].reshape(weight.shape[0], heads * NOPE),
            parts[..., NOPE:NOPE + half].reshape(weight.shape[0], heads * half),
            parts[..., NOPE + half:].reshape(weight.shape[0], heads * half),
        ],
        axis=1,
    )


def swap(values):
    return lax.ppermute(values, "narrow", perm=[(0, 1), (1, 0)])


def body(
    tokens,
    attn_gain,
    q_weight,
    kva_weight,
    kv_gain,
    kvb_weight,
    o_weight,
    adapter_down,
    adapter_up_weight,
    lengths,
    adapter_ids,
    adapter_slot,
):
    rows = tokens.shape[0]
    half_width = tokens.shape[1]
    heads_here = o_weight.shape[0] // VDIM
    prompts_here = lengths.shape[1]
    q_cols = q_weight.shape[1]
    me = lax.axis_index("narrow")
    mine_first = me == 0

    joined = jnp.concatenate([split_heads(q_weight, heads_here), kva_weight], axis=1)
    joined = lax.all_gather(joined, "wide", axis=0, tiled=True)

    other = swap(tokens)
    whole = jnp.concatenate(
        [jnp.where(mine_first, tokens, other), jnp.where(mine_first, other, tokens)], axis=1
    )

    slots_here = adapter_down.shape[1] // RANK
    prompt_ids = adapter_ids[0]
    id_hot = (prompt_ids[:, None] == jnp.arange(adapter_slot.shape[0])[None, :]).astype(jnp.int32)
    prompt_slot = jnp.sum(id_hot * adapter_slot[None, :], axis=1)
    owner = prompt_slot // slots_here
    local_slot = prompt_slot % slots_here
    picked = jnp.concatenate(
        [
            lax.dynamic_slice_in_dim(adapter_down, local_slot[p] * RANK, RANK, 1)
            for p in range(prompts_here)
        ],
        axis=1,
    )
    picked_other = swap(picked)
    own_block = jnp.repeat(owner == me, RANK)
    chosen = jnp.where(own_block[None, :], picked, picked_other)

    normed = rms_scale(whole.astype(jnp.float32), attn_gain).astype(jnp.bfloat16)
    local_pos = jnp.arange(rows)
    prompt, position, adapter, slot = token_tables(
        lengths[0], adapter_ids[0], adapter_slot, local_pos
    )
    projections = jnp.dot(normed, joined, preferred_element_type=jnp.float32)
    query_vectors = projections[:, :q_cols]
    kv_pre = projections[:, q_cols:]
    member = (prompt[:, None] == jnp.arange(prompts_here)[None, :]).astype(jnp.float32)
    low = jnp.dot(normed, chosen, preferred_element_type=jnp.float32).reshape(
        rows, prompts_here, RANK
    )
    lowrank = jnp.sum(low * member[:, :, None], axis=1).astype(jnp.bfloat16)
    up_blocks = [
        lax.dynamic_slice_in_dim(adapter_up_weight, prompt_ids[prompt_index] * RANK, RANK, 0)
        for prompt_index in range(prompts_here)
    ]
    up_weight_rows = split_heads(jnp.concatenate(up_blocks, axis=0), heads_here)
    spread_rows = (member.astype(jnp.bfloat16)[:, :, None] * lowrank[:, None, :]).reshape(
        rows, prompts_here * RANK
    )
    query_vectors = query_vectors + ADAPTER_SCALE * jnp.dot(
        spread_rows, up_weight_rows, preferred_element_type=jnp.float32
    )
    nope_cols = heads_here * NOPE
    half_cols = heads_here * (ROPE // 2)
    q_nope = query_vectors[:, :nope_cols].astype(jnp.bfloat16)
    first = query_vectors[:, nope_cols:nope_cols + half_cols]
    second = query_vectors[:, nope_cols + half_cols:]
    half = ROPE // 2
    freqs = jnp.exp(-jnp.log(THETA) * 2.0 * jnp.arange(half).astype(jnp.float32) / (2 * half))
    angle = position.astype(jnp.float32)[:, None] * freqs[None, :]
    cosine = jnp.tile(jnp.cos(angle), (1, heads_here))
    sine = jnp.tile(jnp.sin(angle), (1, heads_here))
    turned_first = (first * cosine - second * sine).astype(jnp.bfloat16)
    turned_second = (first * sine + second * cosine).astype(jnp.bfloat16)
    q_rope = jnp.transpose(
        jnp.concatenate(
            [
                turned_first.reshape(rows, heads_here, half),
                turned_second.reshape(rows, heads_here, half),
            ],
            axis=-1,
        ),
        (1, 0, 2),
    )
    latent = rms_scale(kv_pre[:, :LATENT], kv_gain).astype(jnp.bfloat16)
    key_rope = rotate(kv_pre[:, LATENT:], position).astype(jnp.bfloat16)
    latent_cache = jnp.concatenate([latent, key_rope], axis=1)
    expanded = jnp.dot(latent, kvb_weight, preferred_element_type=jnp.float32).astype(jnp.bfloat16)
    key_start = (local_pos - position).astype(jnp.int32)
    attended = attend(q_nope, q_rope, expanded, key_rope, key_start)
    their_cols = lax.dynamic_slice_in_dim(o_weight, (1 - me) * half_width, half_width, 1)
    my_cols = lax.dynamic_slice_in_dim(o_weight, me * half_width, half_width, 1)
    theirs = jnp.dot(attended, their_cols, preferred_element_type=jnp.float32).astype(jnp.bfloat16)
    received = swap(theirs)
    mine = jnp.dot(attended, my_cols, preferred_element_type=jnp.float32).astype(jnp.bfloat16)
    projected = mine.astype(jnp.float32) + received.astype(jnp.float32)
    hidden = (tokens.astype(jnp.float32) + projected).astype(jnp.bfloat16)
    return (hidden, latent_cache)


def solution(mesh):
    return jax.shard_map(
        body,
        mesh=mesh,
        in_specs=(
            P("wide", "narrow"),
            P(),
            P("wide", "narrow"),
            P("wide", None),
            P(),
            P(None, "narrow"),
            P("narrow", None),
            P(None, "narrow"),
            P(None, "narrow"),
            P("wide", None),
            P("wide", None),
            P(),
        ),
        out_specs=(P("wide", "narrow"), P("wide", None)),
        check_vma=False,
    )
```

```python
import jax
import jax.numpy as jnp
from jax import lax
from jax.sharding import PartitionSpec as P
from jax.experimental import pallas as pl
from jax.experimental.pallas import tpu as pltpu

NOPE = 128
ROPE = 64
VDIM = 128
LATENT = 512
RANK = 16
LMAX = 512
QBLOCK = 256
WINDOW = QBLOCK + LMAX
PBLOCK = 256


EPS = 1e-06
THETA = 50000.0
ADAPTER_SCALE = 2.0


def rms_scale(values, gain):
    mean_sq = jnp.mean(values * values, axis=-1, keepdims=True)
    return values * lax.rsqrt(mean_sq + EPS) * gain.astype(jnp.float32)


def rotate(values, positions):
    half = values.shape[-1] // 2
    freqs = jnp.exp(-jnp.log(THETA) * 2.0 * jnp.arange(half).astype(jnp.float32) / (2 * half))
    angle = positions.astype(jnp.float32)[:, None] * freqs[None, :]
    cosine = jnp.cos(angle)
    sine = jnp.sin(angle)
    if values.ndim == 3:
        cosine = cosine[:, None, :]
        sine = sine[:, None, :]
    first = values[..., :half]
    second = values[..., half:]
    return jnp.concatenate(
        [first * cosine - second * sine, first * sine + second * cosine], axis=-1
    )


def token_tables(length_row, id_row, adapter_slot, local_pos):
    ends = jnp.cumsum(length_row)
    starts = ends - length_row
    prompt = jnp.sum((ends[None, :] <= local_pos[:, None]).astype(jnp.int32), axis=1)
    onehot = (prompt[:, None] == jnp.arange(length_row.shape[0])[None, :]).astype(jnp.int32)
    position = local_pos - jnp.sum(onehot * starts[None, :], axis=1)
    adapter = jnp.sum(onehot * id_row[None, :], axis=1)
    slot_hot = (adapter[:, None] == jnp.arange(adapter_slot.shape[0])[None, :]).astype(jnp.int32)
    slot = jnp.sum(slot_hot * adapter_slot[None, :], axis=1)
    return (prompt, position, adapter, slot)


def project_kernel(x_ref, w_ref, sp_ref, up_ref, cos_ref, sin_ref, gain_ref, kvb_ref,
                   qn_ref, qf_ref, qs_ref, lat_ref, kr_ref, kv_ref):
    x = x_ref[...]
    sp = sp_ref[...]
    nope = qn_ref.shape[1]
    half = qf_ref.shape[1]

    def query_part(lo, hi):
        base = jnp.dot(x, w_ref[:, lo:hi], preferred_element_type=jnp.float32)
        return base + ADAPTER_SCALE * jnp.dot(sp, up_ref[:, lo:hi], preferred_element_type=jnp.float32)

    qn_ref[...] = query_part(0, nope).astype(qn_ref.dtype)
    first = query_part(nope, nope + half)
    second = query_part(nope + half, nope + 2 * half)
    cosine = cos_ref[...]
    sine = sin_ref[...]
    qf_ref[...] = (first * cosine - second * sine).astype(qf_ref.dtype)
    qs_ref[...] = (first * sine + second * cosine).astype(qs_ref.dtype)
    q_end = nope + 2 * half
    pre = jnp.dot(x, w_ref[:, q_end:q_end + LATENT], preferred_element_type=jnp.float32)
    mean_sq = jnp.mean(pre * pre, axis=-1, keepdims=True)
    latent = (pre * lax.rsqrt(mean_sq + EPS) * gain_ref[...]).astype(jnp.bfloat16)
    lat_ref[...] = latent
    kr_ref[...] = jnp.dot(x, w_ref[:, q_end + LATENT:], preferred_element_type=jnp.float32)
    kv_ref[...] = jnp.dot(latent, kvb_ref[...], preferred_element_type=jnp.float32).astype(kv_ref.dtype)


def project(normed, joined, spread, up_rows, cosine, sine, kv_gain, kvb_weight, heads):
    rows, width = normed.shape
    cols = joined.shape[1]
    half = heads * ROPE // 2
    nope = heads * NOPE
    full = lambda shape: pl.BlockSpec(shape, lambda i: (0, 0))
    part = lambda c: pl.BlockSpec((PBLOCK, c), lambda i: (i, 0))
    return pl.pallas_call(
        project_kernel,
        grid=(rows // PBLOCK,),
        in_specs=[
            part(width), full((width, cols)), part(spread.shape[1]), full(up_rows.shape),
            part(half), part(half), full((1, LATENT)), full(kvb_weight.shape),
        ],
        out_specs=[part(nope), part(half), part(half), part(LATENT), part(ROPE), part(kvb_weight.shape[1])],
        out_shape=[
            jax.ShapeDtypeStruct((rows, nope), jnp.bfloat16),
            jax.ShapeDtypeStruct((rows, half), jnp.bfloat16),
            jax.ShapeDtypeStruct((rows, half), jnp.bfloat16),
            jax.ShapeDtypeStruct((rows, LATENT), jnp.bfloat16),
            jax.ShapeDtypeStruct((rows, ROPE), jnp.float32),
            jax.ShapeDtypeStruct((rows, kvb_weight.shape[1]), jnp.bfloat16),
        ],
    )(normed, joined, spread, up_rows, cosine, sine, kv_gain.astype(jnp.float32)[None, :], kvb_weight)


def attention_kernel(q_nope_ref, qf_ref, qs_ref, kv_ref, kr_ref, kst_ref, o_ref):
    i = pl.program_id(0)
    heads = qf_ref.shape[1] * 2 // ROPE
    half = ROPE // 2
    scale = 1.0 / jnp.sqrt(jnp.float32(NOPE + ROPE))
    start = pl.multiple_of(jnp.maximum(i * QBLOCK - LMAX, 0), 128)
    row = i * QBLOCK + lax.broadcasted_iota(jnp.int32, (QBLOCK, WINDOW), 0)
    col = start + lax.broadcasted_iota(jnp.int32, (QBLOCK, WINDOW), 1)
    allowed = (col >= kst_ref[...]) & (col <= row)
    kr = kr_ref[pl.ds(start, WINDOW), :]
    kf = kr[:, :half]
    ks = kr[:, half:]
    qf_all = qf_ref[...]
    qs_all = qs_ref[...]
    for h in range(heads):
        qn = q_nope_ref[:, h * NOPE:(h + 1) * NOPE]
        qf = qf_all[:, h * half:(h + 1) * half]
        qs = qs_all[:, h * half:(h + 1) * half]
        kn = kv_ref[pl.ds(start, WINDOW), h * (NOPE + VDIM):h * (NOPE + VDIM) + NOPE]
        s = lax.dot_general(qn, kn, (((1,), (1,)), ((), ())), preferred_element_type=jnp.float32)
        rope = lax.dot_general(qf, kf, (((1,), (1,)), ((), ())), preferred_element_type=jnp.float32)
        rope = rope + lax.dot_general(qs, ks, (((1,), (1,)), ((), ())), preferred_element_type=jnp.float32)
        s = jnp.where(allowed, (s + rope) * scale, jnp.float32(-1e30))
        top = jnp.max(s, axis=1, keepdims=True)
        e = jnp.exp(s - top)
        w = (e * (1.0 / jnp.sum(e, axis=1, keepdims=True))).astype(jnp.bfloat16)
        v = kv_ref[pl.ds(start, WINDOW), h * (NOPE + VDIM) + NOPE:(h + 1) * (NOPE + VDIM)]
        o_ref[:, h * VDIM:(h + 1) * VDIM] = jnp.dot(
            w, v, preferred_element_type=jnp.float32
        ).astype(o_ref.dtype)


def attend(q_nope, q_first, q_second, kv, key_rope, key_start):
    rows = q_nope.shape[0]
    heads = q_nope.shape[1] // NOPE
    half = q_first.shape[1]
    return pl.pallas_call(
        attention_kernel,
        grid=(rows // QBLOCK,),
        in_specs=[
            pl.BlockSpec((QBLOCK, heads * NOPE), lambda i: (i, 0)),
            pl.BlockSpec((QBLOCK, half), lambda i: (i, 0)),
            pl.BlockSpec((QBLOCK, half), lambda i: (i, 0)),
            pl.BlockSpec((rows, heads * (NOPE + VDIM)), lambda i: (0, 0)),
            pl.BlockSpec((rows, ROPE), lambda i: (0, 0)),
            pl.BlockSpec((QBLOCK, 1), lambda i: (i, 0)),
        ],
        out_specs=pl.BlockSpec((QBLOCK, heads * VDIM), lambda i: (i, 0)),
        out_shape=jax.ShapeDtypeStruct((rows, heads * VDIM), jnp.bfloat16),
    )(q_nope, q_first, q_second, kv, key_rope, key_start[:, None])


def split_heads(weight, heads):
    parts = weight.reshape(weight.shape[0], heads, NOPE + ROPE)
    half = ROPE // 2
    return jnp.concatenate(
        [
            parts[..., :NOPE].reshape(weight.shape[0], heads * NOPE),
            parts[..., NOPE:NOPE + half].reshape(weight.shape[0], heads * half),
            parts[..., NOPE + half:].reshape(weight.shape[0], heads * half),
        ],
        axis=1,
    )


def swap(values):
    return lax.ppermute(values, "narrow", perm=[(0, 1), (1, 0)])


def body(
    tokens,
    attn_gain,
    q_weight,
    kva_weight,
    kv_gain,
    kvb_weight,
    o_weight,
    adapter_down,
    adapter_up_weight,
    lengths,
    adapter_ids,
    adapter_slot,
):
    rows = tokens.shape[0]
    half_width = tokens.shape[1]
    heads_here = o_weight.shape[0] // VDIM
    prompts_here = lengths.shape[1]
    q_cols = q_weight.shape[1]
    me = lax.axis_index("narrow")
    mine_first = me == 0

    joined = jnp.concatenate([split_heads(q_weight, heads_here), kva_weight], axis=1)
    joined = lax.all_gather(joined, "wide", axis=0, tiled=True)

    other = swap(tokens)
    whole = jnp.concatenate(
        [jnp.where(mine_first, tokens, other), jnp.where(mine_first, other, tokens)], axis=1
    )

    slots_here = adapter_down.shape[1] // RANK
    prompt_ids = adapter_ids[0]
    id_hot = (prompt_ids[:, None] == jnp.arange(adapter_slot.shape[0])[None, :]).astype(jnp.int32)
    prompt_slot = jnp.sum(id_hot * adapter_slot[None, :], axis=1)
    owner = prompt_slot // slots_here
    local_slot = prompt_slot % slots_here
    picked = jnp.concatenate(
        [
            lax.dynamic_slice_in_dim(adapter_down, local_slot[p] * RANK, RANK, 1)
            for p in range(prompts_here)
        ],
        axis=1,
    )
    picked_other = swap(picked)
    own_block = jnp.repeat(owner == me, RANK)
    chosen = jnp.where(own_block[None, :], picked, picked_other)

    normed = rms_scale(whole.astype(jnp.float32), attn_gain).astype(jnp.bfloat16)
    local_pos = jnp.arange(rows)
    prompt, position, adapter, slot = token_tables(
        lengths[0], adapter_ids[0], adapter_slot, local_pos
    )
    member = (prompt[:, None] == jnp.arange(prompts_here)[None, :]).astype(jnp.float32)
    low = jnp.dot(normed, chosen, preferred_element_type=jnp.float32).reshape(
        rows, prompts_here, RANK
    )
    lowrank = jnp.sum(low * member[:, :, None], axis=1).astype(jnp.bfloat16)
    up_blocks = [
        lax.dynamic_slice_in_dim(adapter_up_weight, prompt_ids[prompt_index] * RANK, RANK, 0)
        for prompt_index in range(prompts_here)
    ]
    up_weight_rows = split_heads(jnp.concatenate(up_blocks, axis=0), heads_here)
    spread_rows = (member.astype(jnp.bfloat16)[:, :, None] * lowrank[:, None, :]).reshape(
        rows, prompts_here * RANK
    )
    half = ROPE // 2
    freqs = jnp.exp(-jnp.log(THETA) * 2.0 * jnp.arange(half).astype(jnp.float32) / (2 * half))
    angle = position.astype(jnp.float32)[:, None] * freqs[None, :]
    cosine = jnp.tile(jnp.cos(angle), (1, heads_here))
    sine = jnp.tile(jnp.sin(angle), (1, heads_here))
    q_nope, q_first, q_second, latent, key_pre, expanded = project(
        normed, joined, spread_rows, up_weight_rows, cosine, sine, kv_gain, kvb_weight, heads_here
    )
    key_rope = rotate(key_pre, position).astype(jnp.bfloat16)
    latent_cache = jnp.concatenate([latent, key_rope], axis=1)
    key_start = (local_pos - position).astype(jnp.int32)
    attended = attend(q_nope, q_first, q_second, expanded, key_rope, key_start)
    their_cols = lax.dynamic_slice_in_dim(o_weight, (1 - me) * half_width, half_width, 1)
    my_cols = lax.dynamic_slice_in_dim(o_weight, me * half_width, half_width, 1)
    theirs = jnp.dot(attended, their_cols, preferred_element_type=jnp.float32).astype(jnp.bfloat16)
    received = swap(theirs)
    mine = jnp.dot(attended, my_cols, preferred_element_type=jnp.float32).astype(jnp.bfloat16)
    projected = mine.astype(jnp.float32) + received.astype(jnp.float32)
    hidden = (tokens.astype(jnp.float32) + projected).astype(jnp.bfloat16)
    return (hidden, latent_cache)


def solution(mesh):
    return jax.shard_map(
        body,
        mesh=mesh,
        in_specs=(
            P("wide", "narrow"),
            P(),
            P("wide", "narrow"),
            P("wide", None),
            P(),
            P(None, "narrow"),
            P("narrow", None),
            P(None, "narrow"),
            P(None, "narrow"),
            P("wide", None),
            P("wide", None),
            P(),
        ),
        out_specs=(P("wide", "narrow"), P("wide", None)),
        check_vma=False,
    )
```

```python
import jax
import jax.numpy as jnp
from jax import lax
from jax.sharding import PartitionSpec as P
from jax.experimental import pallas as pl
from jax.experimental.pallas import tpu as pltpu

NOPE = 128
ROPE = 64
VDIM = 128
LATENT = 512
RANK = 16
LMAX = 512
QBLOCK = 256
WINDOW = QBLOCK + LMAX
PBLOCK = 256


EPS = 1e-06
THETA = 50000.0
ADAPTER_SCALE = 2.0


def rms_scale(values, gain):
    mean_sq = jnp.mean(values * values, axis=-1, keepdims=True)
    return values * lax.rsqrt(mean_sq + EPS) * gain.astype(jnp.float32)


def rotate(values, positions):
    half = values.shape[-1] // 2
    freqs = jnp.exp(-jnp.log(THETA) * 2.0 * jnp.arange(half).astype(jnp.float32) / (2 * half))
    angle = positions.astype(jnp.float32)[:, None] * freqs[None, :]
    cosine = jnp.cos(angle)
    sine = jnp.sin(angle)
    if values.ndim == 3:
        cosine = cosine[:, None, :]
        sine = sine[:, None, :]
    first = values[..., :half]
    second = values[..., half:]
    return jnp.concatenate(
        [first * cosine - second * sine, first * sine + second * cosine], axis=-1
    )


def token_tables(length_row, id_row, adapter_slot, local_pos):
    ends = jnp.cumsum(length_row)
    starts = ends - length_row
    prompt = jnp.sum((ends[None, :] <= local_pos[:, None]).astype(jnp.int32), axis=1)
    onehot = (prompt[:, None] == jnp.arange(length_row.shape[0])[None, :]).astype(jnp.int32)
    position = local_pos - jnp.sum(onehot * starts[None, :], axis=1)
    adapter = jnp.sum(onehot * id_row[None, :], axis=1)
    slot_hot = (adapter[:, None] == jnp.arange(adapter_slot.shape[0])[None, :]).astype(jnp.int32)
    slot = jnp.sum(slot_hot * adapter_slot[None, :], axis=1)
    return (prompt, position, adapter, slot)


def project_kernel(x_ref, w_ref, sp_ref, up_ref, cos_ref, sin_ref, gain_ref, kvb_ref,
                   qn_ref, qf_ref, qs_ref, cache_ref, kv_ref):
    x = x_ref[...]
    sp = sp_ref[...]
    nope = qn_ref.shape[1]
    half = qf_ref.shape[1]

    def query_part(lo, hi):
        base = jnp.dot(x, w_ref[:, lo:hi], preferred_element_type=jnp.float32)
        return base + ADAPTER_SCALE * jnp.dot(sp, up_ref[:, lo:hi], preferred_element_type=jnp.float32)

    qn_ref[...] = query_part(0, nope).astype(qn_ref.dtype)
    first = query_part(nope, nope + half)
    second = query_part(nope + half, nope + 2 * half)
    cosine = cos_ref[...]
    sine = sin_ref[...]
    qf_ref[...] = (first * cosine - second * sine).astype(qf_ref.dtype)
    qs_ref[...] = (first * sine + second * cosine).astype(qs_ref.dtype)
    q_end = nope + 2 * half
    pre = jnp.dot(x, w_ref[:, q_end:q_end + LATENT], preferred_element_type=jnp.float32)
    mean_sq = jnp.mean(pre * pre, axis=-1, keepdims=True)
    latent = (pre * lax.rsqrt(mean_sq + EPS) * gain_ref[...]).astype(jnp.bfloat16)
    cache_ref[:, :LATENT] = latent
    key = jnp.dot(x, w_ref[:, q_end + LATENT:], preferred_element_type=jnp.float32)
    key_first = key[:, :ROPE // 2]
    key_second = key[:, ROPE // 2:]
    cosine = cosine[:, :ROPE // 2]
    sine = sine[:, :ROPE // 2]
    cache_ref[:, LATENT:LATENT + ROPE // 2] = (key_first * cosine - key_second * sine).astype(cache_ref.dtype)
    cache_ref[:, LATENT + ROPE // 2:] = (key_first * sine + key_second * cosine).astype(cache_ref.dtype)
    kv_ref[...] = jnp.dot(latent, kvb_ref[...], preferred_element_type=jnp.float32).astype(kv_ref.dtype)


def project(normed, joined, spread, up_rows, cosine, sine, kv_gain, kvb_weight, heads):
    rows, width = normed.shape
    cols = joined.shape[1]
    half = heads * ROPE // 2
    nope = heads * NOPE
    full = lambda shape: pl.BlockSpec(shape, lambda i: (0, 0))
    part = lambda c: pl.BlockSpec((PBLOCK, c), lambda i: (i, 0))
    return pl.pallas_call(
        project_kernel,
        grid=(rows // PBLOCK,),
        in_specs=[
            part(width), full((width, cols)), part(spread.shape[1]), full(up_rows.shape),
            part(half), part(half), full((1, LATENT)), full(kvb_weight.shape),
        ],
        out_specs=[part(nope), part(half), part(half), part(LATENT + ROPE), part(kvb_weight.shape[1])],
        out_shape=[
            jax.ShapeDtypeStruct((rows, nope), jnp.bfloat16),
            jax.ShapeDtypeStruct((rows, half), jnp.bfloat16),
            jax.ShapeDtypeStruct((rows, half), jnp.bfloat16),
            jax.ShapeDtypeStruct((rows, LATENT + ROPE), jnp.bfloat16),
            jax.ShapeDtypeStruct((rows, kvb_weight.shape[1]), jnp.bfloat16),
        ],
    )(normed, joined, spread, up_rows, cosine, sine, kv_gain.astype(jnp.float32)[None, :], kvb_weight)


def attention_kernel(me_ref, q_nope_ref, qf_ref, qs_ref, kv_ref, cache_ref, kst_ref, wt_ref, wm_ref,
                     theirs_ref, mine_ref, att_ref):
    i = pl.program_id(0)
    heads = qf_ref.shape[1] * 2 // ROPE
    half = ROPE // 2
    scale = 1.0 / jnp.sqrt(jnp.float32(NOPE + ROPE))
    start = pl.multiple_of(jnp.maximum(i * QBLOCK - LMAX, 0), 128)
    row = i * QBLOCK + lax.broadcasted_iota(jnp.int32, (QBLOCK, WINDOW), 0)
    col = start + lax.broadcasted_iota(jnp.int32, (QBLOCK, WINDOW), 1)
    allowed = (col >= kst_ref[...]) & (col <= row)
    kr = cache_ref[pl.ds(start, WINDOW), LATENT:LATENT + ROPE]
    kf = kr[:, :half]
    ks = kr[:, half:]
    qf_all = qf_ref[...]
    qs_all = qs_ref[...]
    for h in range(heads):
        qn = q_nope_ref[:, h * NOPE:(h + 1) * NOPE]
        qf = qf_all[:, h * half:(h + 1) * half]
        qs = qs_all[:, h * half:(h + 1) * half]
        kn = kv_ref[pl.ds(start, WINDOW), h * (NOPE + VDIM):h * (NOPE + VDIM) + NOPE]
        s = lax.dot_general(qn, kn, (((1,), (1,)), ((), ())), preferred_element_type=jnp.float32)
        rope = lax.dot_general(qf, kf, (((1,), (1,)), ((), ())), preferred_element_type=jnp.float32)
        rope = rope + lax.dot_general(qs, ks, (((1,), (1,)), ((), ())), preferred_element_type=jnp.float32)
        s = jnp.where(allowed, (s + rope) * scale, jnp.float32(-1e30))
        top = jnp.max(s, axis=1, keepdims=True)
        e = jnp.exp(s - top)
        w = (e * (1.0 / jnp.sum(e, axis=1, keepdims=True))).astype(jnp.bfloat16)
        v = kv_ref[pl.ds(start, WINDOW), h * (NOPE + VDIM) + NOPE:(h + 1) * (NOPE + VDIM)]
        att_ref[:, h * VDIM:(h + 1) * VDIM] = jnp.dot(
            w, v, preferred_element_type=jnp.float32
        ).astype(att_ref.dtype)
    att = att_ref[...]
    theirs_ref[...] = jnp.dot(att, wt_ref[...], preferred_element_type=jnp.float32).astype(theirs_ref.dtype)
    mine_ref[...] = jnp.dot(att, wm_ref[...], preferred_element_type=jnp.float32).astype(mine_ref.dtype)


def attend(me, q_nope, q_first, q_second, kv, latent_cache, key_start, o_weight):
    rows = q_nope.shape[0]
    heads = q_nope.shape[1] // NOPE
    half = q_first.shape[1]
    out_half = o_weight.shape[1] // 2
    grid_spec = pltpu.PrefetchScalarGridSpec(
        num_scalar_prefetch=1,
        grid=(rows // QBLOCK,),
        in_specs=[
            pl.BlockSpec((QBLOCK, heads * NOPE), lambda i, m: (i, 0)),
            pl.BlockSpec((QBLOCK, half), lambda i, m: (i, 0)),
            pl.BlockSpec((QBLOCK, half), lambda i, m: (i, 0)),
            pl.BlockSpec((rows, heads * (NOPE + VDIM)), lambda i, m: (0, 0)),
            pl.BlockSpec((rows, LATENT + ROPE), lambda i, m: (0, 0)),
            pl.BlockSpec((QBLOCK, 1), lambda i, m: (i, 0)),
            pl.BlockSpec((heads * VDIM, out_half), lambda i, m: (0, 1 - m[0])),
            pl.BlockSpec((heads * VDIM, out_half), lambda i, m: (0, m[0])),
        ],
        out_specs=[
            pl.BlockSpec((QBLOCK, out_half), lambda i, m: (i, 0)),
            pl.BlockSpec((QBLOCK, out_half), lambda i, m: (i, 0)),
        ],
        scratch_shapes=[pltpu.VMEM((QBLOCK, heads * VDIM), jnp.bfloat16)],
    )
    return pl.pallas_call(
        attention_kernel,
        grid_spec=grid_spec,
        out_shape=[
            jax.ShapeDtypeStruct((rows, out_half), jnp.bfloat16),
            jax.ShapeDtypeStruct((rows, out_half), jnp.bfloat16),
        ],
    )(me, q_nope, q_first, q_second, kv, latent_cache, key_start[:, None], o_weight, o_weight)


def split_heads(weight, heads):
    parts = weight.reshape(weight.shape[0], heads, NOPE + ROPE)
    half = ROPE // 2
    return jnp.concatenate(
        [
            parts[..., :NOPE].reshape(weight.shape[0], heads * NOPE),
            parts[..., NOPE:NOPE + half].reshape(weight.shape[0], heads * half),
            parts[..., NOPE + half:].reshape(weight.shape[0], heads * half),
        ],
        axis=1,
    )


def swap(values):
    return lax.ppermute(values, "narrow", perm=[(0, 1), (1, 0)])


def body(
    tokens,
    attn_gain,
    q_weight,
    kva_weight,
    kv_gain,
    kvb_weight,
    o_weight,
    adapter_down,
    adapter_up_weight,
    lengths,
    adapter_ids,
    adapter_slot,
):
    rows = tokens.shape[0]
    half_width = tokens.shape[1]
    heads_here = o_weight.shape[0] // VDIM
    prompts_here = lengths.shape[1]
    q_cols = q_weight.shape[1]
    me = lax.axis_index("narrow")
    mine_first = me == 0

    joined = jnp.concatenate([split_heads(q_weight, heads_here), kva_weight], axis=1)
    joined = lax.all_gather(joined, "wide", axis=0, tiled=True)

    other = swap(tokens)
    whole = jnp.concatenate(
        [jnp.where(mine_first, tokens, other), jnp.where(mine_first, other, tokens)], axis=1
    )

    slots_here = adapter_down.shape[1] // RANK
    prompt_ids = adapter_ids[0]
    id_hot = (prompt_ids[:, None] == jnp.arange(adapter_slot.shape[0])[None, :]).astype(jnp.int32)
    prompt_slot = jnp.sum(id_hot * adapter_slot[None, :], axis=1)
    owner = prompt_slot // slots_here
    local_slot = prompt_slot % slots_here
    picked = jnp.concatenate(
        [
            lax.dynamic_slice_in_dim(adapter_down, local_slot[p] * RANK, RANK, 1)
            for p in range(prompts_here)
        ],
        axis=1,
    )
    picked_other = swap(picked)
    own_block = jnp.repeat(owner == me, RANK)
    chosen = jnp.where(own_block[None, :], picked, picked_other)

    normed = rms_scale(whole.astype(jnp.float32), attn_gain).astype(jnp.bfloat16)
    local_pos = jnp.arange(rows)
    prompt, position, adapter, slot = token_tables(
        lengths[0], adapter_ids[0], adapter_slot, local_pos
    )
    member = (prompt[:, None] == jnp.arange(prompts_here)[None, :]).astype(jnp.float32)
    low = jnp.dot(normed, chosen, preferred_element_type=jnp.float32).reshape(
        rows, prompts_here, RANK
    )
    lowrank = jnp.sum(low * member[:, :, None], axis=1).astype(jnp.bfloat16)
    up_blocks = [
        lax.dynamic_slice_in_dim(adapter_up_weight, prompt_ids[prompt_index] * RANK, RANK, 0)
        for prompt_index in range(prompts_here)
    ]
    up_weight_rows = split_heads(jnp.concatenate(up_blocks, axis=0), heads_here)
    spread_rows = (member.astype(jnp.bfloat16)[:, :, None] * lowrank[:, None, :]).reshape(
        rows, prompts_here * RANK
    )
    half = ROPE // 2
    freqs = jnp.exp(-jnp.log(THETA) * 2.0 * jnp.arange(half).astype(jnp.float32) / (2 * half))
    angle = position.astype(jnp.float32)[:, None] * freqs[None, :]
    cosine = jnp.tile(jnp.cos(angle), (1, heads_here))
    sine = jnp.tile(jnp.sin(angle), (1, heads_here))
    q_nope, q_first, q_second, latent_cache, expanded = project(
        normed, joined, spread_rows, up_weight_rows, cosine, sine, kv_gain, kvb_weight, heads_here
    )
    key_start = (local_pos - position).astype(jnp.int32)
    theirs, mine = attend(
        me.astype(jnp.int32).reshape(1), q_nope, q_first, q_second, expanded, latent_cache,
        key_start, o_weight,
    )
    received = swap(theirs)
    projected = mine.astype(jnp.float32) + received.astype(jnp.float32)
    hidden = (tokens.astype(jnp.float32) + projected).astype(jnp.bfloat16)
    return (hidden, latent_cache)


def solution(mesh):
    return jax.shard_map(
        body,
        mesh=mesh,
        in_specs=(
            P("wide", "narrow"),
            P(),
            P("wide", "narrow"),
            P("wide", None),
            P(),
            P(None, "narrow"),
            P("narrow", None),
            P(None, "narrow"),
            P(None, "narrow"),
            P("wide", None),
            P("wide", None),
            P(),
        ),
        out_specs=(P("wide", "narrow"), P("wide", None)),
        check_vma=False,
    )
```

```python
import jax
import jax.numpy as jnp
from jax import lax
from jax.sharding import PartitionSpec as P
from jax.experimental import pallas as pl
from jax.experimental.pallas import tpu as pltpu

NOPE = 128
ROPE = 64
VDIM = 128
LATENT = 512
RANK = 16
LMAX = 512
QBLOCK = 256
WINDOW = QBLOCK + LMAX
PBLOCK = 256


EPS = 1e-06
THETA = 50000.0
ADAPTER_SCALE = 2.0


def rms_scale(values, gain):
    mean_sq = jnp.mean(values * values, axis=-1, keepdims=True)
    return values * lax.rsqrt(mean_sq + EPS) * gain.astype(jnp.float32)


def rotate(values, positions):
    half = values.shape[-1] // 2
    freqs = jnp.exp(-jnp.log(THETA) * 2.0 * jnp.arange(half).astype(jnp.float32) / (2 * half))
    angle = positions.astype(jnp.float32)[:, None] * freqs[None, :]
    cosine = jnp.cos(angle)
    sine = jnp.sin(angle)
    if values.ndim == 3:
        cosine = cosine[:, None, :]
        sine = sine[:, None, :]
    first = values[..., :half]
    second = values[..., half:]
    return jnp.concatenate(
        [first * cosine - second * sine, first * sine + second * cosine], axis=-1
    )


def token_tables(length_row, id_row, adapter_slot, local_pos):
    ends = jnp.cumsum(length_row)
    starts = ends - length_row
    prompt = jnp.sum((ends[None, :] <= local_pos[:, None]).astype(jnp.int32), axis=1)
    onehot = (prompt[:, None] == jnp.arange(length_row.shape[0])[None, :]).astype(jnp.int32)
    position = local_pos - jnp.sum(onehot * starts[None, :], axis=1)
    adapter = jnp.sum(onehot * id_row[None, :], axis=1)
    slot_hot = (adapter[:, None] == jnp.arange(adapter_slot.shape[0])[None, :]).astype(jnp.int32)
    slot = jnp.sum(slot_hot * adapter_slot[None, :], axis=1)
    return (prompt, position, adapter, slot)


def project_kernel(x_ref, w_ref, sp_ref, up_ref, cos_ref, sin_ref, gain_ref, kvb_ref,
                   qn_ref, qf_ref, qs_ref, cache_ref, kv_ref):
    x = x_ref[...]
    sp = sp_ref[...]
    nope = qn_ref.shape[1]
    half = qf_ref.shape[1]

    def query_part(lo, hi):
        base = jnp.dot(x, w_ref[:, lo:hi], preferred_element_type=jnp.float32)
        return base + ADAPTER_SCALE * jnp.dot(sp, up_ref[:, lo:hi], preferred_element_type=jnp.float32)

    qn_ref[...] = query_part(0, nope).astype(qn_ref.dtype)
    first = query_part(nope, nope + half)
    second = query_part(nope + half, nope + 2 * half)
    cosine = cos_ref[...]
    sine = sin_ref[...]
    qf_ref[...] = (first * cosine - second * sine).astype(qf_ref.dtype)
    qs_ref[...] = (first * sine + second * cosine).astype(qs_ref.dtype)
    q_end = nope + 2 * half
    pre = jnp.dot(x, w_ref[:, q_end:q_end + LATENT], preferred_element_type=jnp.float32)
    mean_sq = jnp.mean(pre * pre, axis=-1, keepdims=True)
    latent = (pre * lax.rsqrt(mean_sq + EPS) * gain_ref[...]).astype(jnp.bfloat16)
    cache_ref[:, :LATENT] = latent
    key = jnp.dot(x, w_ref[:, q_end + LATENT:], preferred_element_type=jnp.float32)
    key_first = key[:, :ROPE // 2]
    key_second = key[:, ROPE // 2:]
    cosine = cosine[:, :ROPE // 2]
    sine = sine[:, :ROPE // 2]
    cache_ref[:, LATENT:LATENT + ROPE // 2] = (key_first * cosine - key_second * sine).astype(cache_ref.dtype)
    cache_ref[:, LATENT + ROPE // 2:] = (key_first * sine + key_second * cosine).astype(cache_ref.dtype)
    kv_ref[...] = jnp.dot(latent, kvb_ref[...], preferred_element_type=jnp.float32).astype(kv_ref.dtype)


def project(normed, joined, spread, up_rows, cosine, sine, kv_gain, kvb_weight, heads):
    rows, width = normed.shape
    cols = joined.shape[1]
    half = heads * ROPE // 2
    nope = heads * NOPE
    full = lambda shape: pl.BlockSpec(shape, lambda i: (0, 0))
    part = lambda c: pl.BlockSpec((PBLOCK, c), lambda i: (i, 0))
    return pl.pallas_call(
        project_kernel,
        grid=(rows // PBLOCK,),
        in_specs=[
            part(width), full((width, cols)), part(spread.shape[1]), full(up_rows.shape),
            part(half), part(half), full((1, LATENT)), full(kvb_weight.shape),
        ],
        out_specs=[part(nope), part(half), part(half), part(LATENT + ROPE), part(kvb_weight.shape[1])],
        out_shape=[
            jax.ShapeDtypeStruct((rows, nope), jnp.bfloat16),
            jax.ShapeDtypeStruct((rows, half), jnp.bfloat16),
            jax.ShapeDtypeStruct((rows, half), jnp.bfloat16),
            jax.ShapeDtypeStruct((rows, LATENT + ROPE), jnp.bfloat16),
            jax.ShapeDtypeStruct((rows, kvb_weight.shape[1]), jnp.bfloat16),
        ],
    )(normed, joined, spread, up_rows, cosine, sine, kv_gain.astype(jnp.float32)[None, :], kvb_weight)


def attention_kernel(me_ref, first_ref, q_nope_ref, qf_ref, qs_ref, kv_ref, cache_ref, kst_ref, wt_ref,
                     wm_ref, theirs_ref, mine_ref, att_ref):
    i = pl.program_id(0)
    heads = qf_ref.shape[1] * 2 // ROPE
    half = ROPE // 2
    scale = 1.0 / jnp.sqrt(jnp.float32(NOPE + ROPE))
    qf_all = qf_ref[...]
    qs_all = qs_ref[...]
    kst = kst_ref[...]

    def run(start, width):
        start = pl.multiple_of(start, 128)
        row = i * QBLOCK + lax.broadcasted_iota(jnp.int32, (QBLOCK, width), 0)
        col = start + lax.broadcasted_iota(jnp.int32, (QBLOCK, width), 1)
        allowed = (col >= kst) & (col <= row)
        kr = cache_ref[pl.ds(start, width), LATENT:LATENT + ROPE]
        kf = kr[:, :half]
        ks = kr[:, half:]
        for h in range(heads):
            qn = q_nope_ref[:, h * NOPE:(h + 1) * NOPE]
            qf = qf_all[:, h * half:(h + 1) * half]
            qs = qs_all[:, h * half:(h + 1) * half]
            kn = kv_ref[pl.ds(start, width), h * (NOPE + VDIM):h * (NOPE + VDIM) + NOPE]
            s = lax.dot_general(qn, kn, (((1,), (1,)), ((), ())), preferred_element_type=jnp.float32)
            rope = lax.dot_general(qf, kf, (((1,), (1,)), ((), ())), preferred_element_type=jnp.float32)
            rope = rope + lax.dot_general(qs, ks, (((1,), (1,)), ((), ())), preferred_element_type=jnp.float32)
            s = jnp.where(allowed, (s + rope) * scale, jnp.float32(-1e30))
            top = jnp.max(s, axis=1, keepdims=True)
            e = jnp.exp(s - top)
            w = (e * (1.0 / jnp.sum(e, axis=1, keepdims=True))).astype(jnp.bfloat16)
            v = kv_ref[pl.ds(start, width), h * (NOPE + VDIM) + NOPE:(h + 1) * (NOPE + VDIM)]
            att_ref[:, h * VDIM:(h + 1) * VDIM] = jnp.dot(
                w, v, preferred_element_type=jnp.float32
            ).astype(att_ref.dtype)

    first = first_ref[i]
    one = first >= i * QBLOCK
    two = jnp.logical_and(jnp.logical_not(one), first >= i * QBLOCK - QBLOCK)

    @pl.when(one)
    def _():
        run(i * QBLOCK, QBLOCK)

    @pl.when(two)
    def _():
        run(jnp.maximum(i * QBLOCK - QBLOCK, 0), 2 * QBLOCK)

    @pl.when(jnp.logical_not(jnp.logical_or(one, two)))
    def _():
        run(jnp.maximum(i * QBLOCK - LMAX, 0), WINDOW)

    att = att_ref[...]
    theirs_ref[...] = jnp.dot(att, wt_ref[...], preferred_element_type=jnp.float32).astype(theirs_ref.dtype)
    mine_ref[...] = jnp.dot(att, wm_ref[...], preferred_element_type=jnp.float32).astype(mine_ref.dtype)


def attend(me, q_nope, q_first, q_second, kv, latent_cache, key_start, o_weight):
    rows = q_nope.shape[0]
    heads = q_nope.shape[1] // NOPE
    half = q_first.shape[1]
    out_half = o_weight.shape[1] // 2
    grid_spec = pltpu.PrefetchScalarGridSpec(
        num_scalar_prefetch=2,
        grid=(rows // QBLOCK,),
        in_specs=[
            pl.BlockSpec((QBLOCK, heads * NOPE), lambda i, m, f: (i, 0)),
            pl.BlockSpec((QBLOCK, half), lambda i, m, f: (i, 0)),
            pl.BlockSpec((QBLOCK, half), lambda i, m, f: (i, 0)),
            pl.BlockSpec((rows, heads * (NOPE + VDIM)), lambda i, m, f: (0, 0)),
            pl.BlockSpec((rows, LATENT + ROPE), lambda i, m, f: (0, 0)),
            pl.BlockSpec((QBLOCK, 1), lambda i, m, f: (i, 0)),
            pl.BlockSpec((heads * VDIM, out_half), lambda i, m, f: (0, 1 - m[0])),
            pl.BlockSpec((heads * VDIM, out_half), lambda i, m, f: (0, m[0])),
        ],
        out_specs=[
            pl.BlockSpec((QBLOCK, out_half), lambda i, m, f: (i, 0)),
            pl.BlockSpec((QBLOCK, out_half), lambda i, m, f: (i, 0)),
        ],
        scratch_shapes=[pltpu.VMEM((QBLOCK, heads * VDIM), jnp.bfloat16)],
    )
    return pl.pallas_call(
        attention_kernel,
        grid_spec=grid_spec,
        out_shape=[
            jax.ShapeDtypeStruct((rows, out_half), jnp.bfloat16),
            jax.ShapeDtypeStruct((rows, out_half), jnp.bfloat16),
        ],
    )(me, key_start[::QBLOCK], q_nope, q_first, q_second, kv, latent_cache, key_start[:, None], o_weight, o_weight)


def split_heads(weight, heads):
    parts = weight.reshape(weight.shape[0], heads, NOPE + ROPE)
    half = ROPE // 2
    return jnp.concatenate(
        [
            parts[..., :NOPE].reshape(weight.shape[0], heads * NOPE),
            parts[..., NOPE:NOPE + half].reshape(weight.shape[0], heads * half),
            parts[..., NOPE + half:].reshape(weight.shape[0], heads * half),
        ],
        axis=1,
    )


def swap(values):
    return lax.ppermute(values, "narrow", perm=[(0, 1), (1, 0)])


def body(
    tokens,
    attn_gain,
    q_weight,
    kva_weight,
    kv_gain,
    kvb_weight,
    o_weight,
    adapter_down,
    adapter_up_weight,
    lengths,
    adapter_ids,
    adapter_slot,
):
    rows = tokens.shape[0]
    half_width = tokens.shape[1]
    heads_here = o_weight.shape[0] // VDIM
    prompts_here = lengths.shape[1]
    q_cols = q_weight.shape[1]
    me = lax.axis_index("narrow")
    mine_first = me == 0

    joined = jnp.concatenate([split_heads(q_weight, heads_here), kva_weight], axis=1)
    joined = lax.all_gather(joined, "wide", axis=0, tiled=True)

    other = swap(tokens)
    whole = jnp.concatenate(
        [jnp.where(mine_first, tokens, other), jnp.where(mine_first, other, tokens)], axis=1
    )

    slots_here = adapter_down.shape[1] // RANK
    prompt_ids = adapter_ids[0]
    id_hot = (prompt_ids[:, None] == jnp.arange(adapter_slot.shape[0])[None, :]).astype(jnp.int32)
    prompt_slot = jnp.sum(id_hot * adapter_slot[None, :], axis=1)
    owner = prompt_slot // slots_here
    local_slot = prompt_slot % slots_here
    picked = jnp.concatenate(
        [
            lax.dynamic_slice_in_dim(adapter_down, local_slot[p] * RANK, RANK, 1)
            for p in range(prompts_here)
        ],
        axis=1,
    )
    picked_other = swap(picked)
    own_block = jnp.repeat(owner == me, RANK)
    chosen = jnp.where(own_block[None, :], picked, picked_other)

    normed = rms_scale(whole.astype(jnp.float32), attn_gain).astype(jnp.bfloat16)
    local_pos = jnp.arange(rows)
    prompt, position, adapter, slot = token_tables(
        lengths[0], adapter_ids[0], adapter_slot, local_pos
    )
    member = (prompt[:, None] == jnp.arange(prompts_here)[None, :]).astype(jnp.float32)
    low = jnp.dot(normed, chosen, preferred_element_type=jnp.float32).reshape(
        rows, prompts_here, RANK
    )
    lowrank = jnp.sum(low * member[:, :, None], axis=1).astype(jnp.bfloat16)
    up_blocks = [
        lax.dynamic_slice_in_dim(adapter_up_weight, prompt_ids[prompt_index] * RANK, RANK, 0)
        for prompt_index in range(prompts_here)
    ]
    up_weight_rows = split_heads(jnp.concatenate(up_blocks, axis=0), heads_here)
    spread_rows = (member.astype(jnp.bfloat16)[:, :, None] * lowrank[:, None, :]).reshape(
        rows, prompts_here * RANK
    )
    half = ROPE // 2
    freqs = jnp.exp(-jnp.log(THETA) * 2.0 * jnp.arange(half).astype(jnp.float32) / (2 * half))
    angle = position.astype(jnp.float32)[:, None] * freqs[None, :]
    cosine = jnp.tile(jnp.cos(angle), (1, heads_here))
    sine = jnp.tile(jnp.sin(angle), (1, heads_here))
    q_nope, q_first, q_second, latent_cache, expanded = project(
        normed, joined, spread_rows, up_weight_rows, cosine, sine, kv_gain, kvb_weight, heads_here
    )
    key_start = (local_pos - position).astype(jnp.int32)
    theirs, mine = attend(
        me.astype(jnp.int32).reshape(1), q_nope, q_first, q_second, expanded, latent_cache,
        key_start, o_weight,
    )
    received = swap(theirs)
    projected = mine.astype(jnp.float32) + received.astype(jnp.float32)
    hidden = (tokens.astype(jnp.float32) + projected).astype(jnp.bfloat16)
    return (hidden, latent_cache)


def solution(mesh):
    return jax.shard_map(
        body,
        mesh=mesh,
        in_specs=(
            P("wide", "narrow"),
            P(),
            P("wide", "narrow"),
            P("wide", None),
            P(),
            P(None, "narrow"),
            P("narrow", None),
            P(None, "narrow"),
            P(None, "narrow"),
            P("wide", None),
            P("wide", None),
            P(),
        ),
        out_specs=(P("wide", "narrow"), P("wide", None)),
        check_vma=False,
    )
```

```python
import jax
import jax.numpy as jnp
from jax import lax
from jax.sharding import PartitionSpec as P
from jax.experimental import pallas as pl
from jax.experimental.pallas import tpu as pltpu

NOPE = 128
ROPE = 64
VDIM = 128
LATENT = 512
RANK = 16
LMAX = 512
QBLOCK = 256
WINDOW = QBLOCK + LMAX
PBLOCK = 256


EPS = 1e-06
THETA = 50000.0
ADAPTER_SCALE = 2.0


def rms_scale(values, gain):
    mean_sq = jnp.mean(values * values, axis=-1, keepdims=True)
    return values * lax.rsqrt(mean_sq + EPS) * gain.astype(jnp.float32)


def rotate(values, positions):
    half = values.shape[-1] // 2
    freqs = jnp.exp(-jnp.log(THETA) * 2.0 * jnp.arange(half).astype(jnp.float32) / (2 * half))
    angle = positions.astype(jnp.float32)[:, None] * freqs[None, :]
    cosine = jnp.cos(angle)
    sine = jnp.sin(angle)
    if values.ndim == 3:
        cosine = cosine[:, None, :]
        sine = sine[:, None, :]
    first = values[..., :half]
    second = values[..., half:]
    return jnp.concatenate(
        [first * cosine - second * sine, first * sine + second * cosine], axis=-1
    )


def token_tables(length_row, id_row, adapter_slot, local_pos):
    ends = jnp.cumsum(length_row)
    starts = ends - length_row
    prompt = jnp.sum((ends[None, :] <= local_pos[:, None]).astype(jnp.int32), axis=1)
    onehot = (prompt[:, None] == jnp.arange(length_row.shape[0])[None, :]).astype(jnp.int32)
    position = local_pos - jnp.sum(onehot * starts[None, :], axis=1)
    adapter = jnp.sum(onehot * id_row[None, :], axis=1)
    slot_hot = (adapter[:, None] == jnp.arange(adapter_slot.shape[0])[None, :]).astype(jnp.int32)
    slot = jnp.sum(slot_hot * adapter_slot[None, :], axis=1)
    return (prompt, position, adapter, slot)


def project_kernel(x_ref, w_ref, sp_ref, up_ref, cos_ref, sin_ref, gain_ref, kvb_ref,
                   qn_ref, qr_ref, cache_ref, kv_ref):
    x = x_ref[...]
    sp = sp_ref[...]
    nope = qn_ref.shape[1]
    heads = qr_ref.shape[0]
    half = heads * ROPE // 2

    def query_part(lo, hi):
        base = jnp.dot(x, w_ref[:, lo:hi], preferred_element_type=jnp.float32)
        return base + ADAPTER_SCALE * jnp.dot(sp, up_ref[:, lo:hi], preferred_element_type=jnp.float32)

    qn_ref[...] = query_part(0, nope).astype(qn_ref.dtype)
    first = query_part(nope, nope + half)
    second = query_part(nope + half, nope + 2 * half)
    cosine = cos_ref[...]
    sine = sin_ref[...]
    turned_first = (first * cosine - second * sine).astype(qr_ref.dtype)
    turned_second = (first * sine + second * cosine).astype(qr_ref.dtype)
    width = ROPE // 2
    for h in range(heads):
        qr_ref[h, :, :width] = turned_first[:, h * width:(h + 1) * width]
        qr_ref[h, :, width:] = turned_second[:, h * width:(h + 1) * width]
    q_end = nope + 2 * half
    pre = jnp.dot(x, w_ref[:, q_end:q_end + LATENT], preferred_element_type=jnp.float32)
    mean_sq = jnp.mean(pre * pre, axis=-1, keepdims=True)
    latent = (pre * lax.rsqrt(mean_sq + EPS) * gain_ref[...]).astype(jnp.bfloat16)
    cache_ref[:, :LATENT] = latent
    key = jnp.dot(x, w_ref[:, q_end + LATENT:], preferred_element_type=jnp.float32)
    key_first = key[:, :ROPE // 2]
    key_second = key[:, ROPE // 2:]
    cosine = cosine[:, :ROPE // 2]
    sine = sine[:, :ROPE // 2]
    cache_ref[:, LATENT:LATENT + ROPE // 2] = (key_first * cosine - key_second * sine).astype(cache_ref.dtype)
    cache_ref[:, LATENT + ROPE // 2:] = (key_first * sine + key_second * cosine).astype(cache_ref.dtype)
    kv_ref[...] = jnp.dot(latent, kvb_ref[...], preferred_element_type=jnp.float32).astype(kv_ref.dtype)


def project(normed, joined, spread, up_rows, cosine, sine, kv_gain, kvb_weight, heads):
    rows, width = normed.shape
    cols = joined.shape[1]
    half = heads * ROPE // 2
    nope = heads * NOPE
    full = lambda shape: pl.BlockSpec(shape, lambda i: (0, 0))
    part = lambda c: pl.BlockSpec((PBLOCK, c), lambda i: (i, 0))
    return pl.pallas_call(
        project_kernel,
        grid=(rows // PBLOCK,),
        in_specs=[
            part(width), full((width, cols)), part(spread.shape[1]), full(up_rows.shape),
            part(half), part(half), full((1, LATENT)), full(kvb_weight.shape),
        ],
        out_specs=[
            part(nope),
            pl.BlockSpec((heads, PBLOCK, ROPE), lambda i: (0, i, 0)),
            part(LATENT + ROPE),
            part(kvb_weight.shape[1]),
        ],
        out_shape=[
            jax.ShapeDtypeStruct((rows, nope), jnp.bfloat16),
            jax.ShapeDtypeStruct((heads, rows, ROPE), jnp.bfloat16),
            jax.ShapeDtypeStruct((rows, LATENT + ROPE), jnp.bfloat16),
            jax.ShapeDtypeStruct((rows, kvb_weight.shape[1]), jnp.bfloat16),
        ],
    )(normed, joined, spread, up_rows, cosine, sine, kv_gain.astype(jnp.float32)[None, :], kvb_weight)


def attention_kernel(me_ref, first_ref, q_nope_ref, qr_ref, kv_ref, cache_ref, kst_ref, wt_ref,
                     wm_ref, theirs_ref, mine_ref, att_ref):
    i = pl.program_id(0)
    heads = qr_ref.shape[0]
    scale = 1.0 / jnp.sqrt(jnp.float32(NOPE + ROPE))
    kst = kst_ref[...]

    def run(start, width):
        start = pl.multiple_of(start, 128)
        row = i * QBLOCK + lax.broadcasted_iota(jnp.int32, (QBLOCK, width), 0)
        col = start + lax.broadcasted_iota(jnp.int32, (QBLOCK, width), 1)
        allowed = (col >= kst) & (col <= row)
        kr = cache_ref[pl.ds(start, width), LATENT:LATENT + ROPE]
        for h in range(heads):
            qn = q_nope_ref[:, h * NOPE:(h + 1) * NOPE]
            qr = qr_ref[h]
            kn = kv_ref[pl.ds(start, width), h * (NOPE + VDIM):h * (NOPE + VDIM) + NOPE]
            s = lax.dot_general(qn, kn, (((1,), (1,)), ((), ())), preferred_element_type=jnp.float32)
            rope = lax.dot_general(qr, kr, (((1,), (1,)), ((), ())), preferred_element_type=jnp.float32)
            s = jnp.where(allowed, (s + rope) * scale, jnp.float32(-1e30))
            top = jnp.max(s, axis=1, keepdims=True)
            e = jnp.exp(s - top)
            w = (e * (1.0 / jnp.sum(e, axis=1, keepdims=True))).astype(jnp.bfloat16)
            v = kv_ref[pl.ds(start, width), h * (NOPE + VDIM) + NOPE:(h + 1) * (NOPE + VDIM)]
            att_ref[:, h * VDIM:(h + 1) * VDIM] = jnp.dot(
                w, v, preferred_element_type=jnp.float32
            ).astype(att_ref.dtype)

    first = first_ref[i]
    one = first >= i * QBLOCK
    two = jnp.logical_and(jnp.logical_not(one), first >= i * QBLOCK - QBLOCK)

    @pl.when(one)
    def _():
        run(i * QBLOCK, QBLOCK)

    @pl.when(two)
    def _():
        run(jnp.maximum(i * QBLOCK - QBLOCK, 0), 2 * QBLOCK)

    @pl.when(jnp.logical_not(jnp.logical_or(one, two)))
    def _():
        run(jnp.maximum(i * QBLOCK - LMAX, 0), WINDOW)

    att = att_ref[...]
    theirs_ref[...] = jnp.dot(att, wt_ref[...], preferred_element_type=jnp.float32).astype(theirs_ref.dtype)
    mine_ref[...] = jnp.dot(att, wm_ref[...], preferred_element_type=jnp.float32).astype(mine_ref.dtype)


def attend(me, q_nope, q_rope, kv, latent_cache, key_start, o_weight):
    rows = q_nope.shape[0]
    heads = q_nope.shape[1] // NOPE
    out_half = o_weight.shape[1] // 2
    grid_spec = pltpu.PrefetchScalarGridSpec(
        num_scalar_prefetch=2,
        grid=(rows // QBLOCK,),
        in_specs=[
            pl.BlockSpec((QBLOCK, heads * NOPE), lambda i, m, f: (i, 0)),
            pl.BlockSpec((heads, QBLOCK, ROPE), lambda i, m, f: (0, i, 0)),
            pl.BlockSpec((rows, heads * (NOPE + VDIM)), lambda i, m, f: (0, 0)),
            pl.BlockSpec((rows, LATENT + ROPE), lambda i, m, f: (0, 0)),
            pl.BlockSpec((QBLOCK, 1), lambda i, m, f: (i, 0)),
            pl.BlockSpec((heads * VDIM, out_half), lambda i, m, f: (0, 1 - m[0])),
            pl.BlockSpec((heads * VDIM, out_half), lambda i, m, f: (0, m[0])),
        ],
        out_specs=[
            pl.BlockSpec((QBLOCK, out_half), lambda i, m, f: (i, 0)),
            pl.BlockSpec((QBLOCK, out_half), lambda i, m, f: (i, 0)),
        ],
        scratch_shapes=[pltpu.VMEM((QBLOCK, heads * VDIM), jnp.bfloat16)],
    )
    return pl.pallas_call(
        attention_kernel,
        grid_spec=grid_spec,
        out_shape=[
            jax.ShapeDtypeStruct((rows, out_half), jnp.bfloat16),
            jax.ShapeDtypeStruct((rows, out_half), jnp.bfloat16),
        ],
    )(me, key_start[::QBLOCK], q_nope, q_rope, kv, latent_cache, key_start[:, None], o_weight, o_weight)


def split_heads(weight, heads):
    parts = weight.reshape(weight.shape[0], heads, NOPE + ROPE)
    half = ROPE // 2
    return jnp.concatenate(
        [
            parts[..., :NOPE].reshape(weight.shape[0], heads * NOPE),
            parts[..., NOPE:NOPE + half].reshape(weight.shape[0], heads * half),
            parts[..., NOPE + half:].reshape(weight.shape[0], heads * half),
        ],
        axis=1,
    )


def swap(values):
    return lax.ppermute(values, "narrow", perm=[(0, 1), (1, 0)])


def body(
    tokens,
    attn_gain,
    q_weight,
    kva_weight,
    kv_gain,
    kvb_weight,
    o_weight,
    adapter_down,
    adapter_up_weight,
    lengths,
    adapter_ids,
    adapter_slot,
):
    rows = tokens.shape[0]
    half_width = tokens.shape[1]
    heads_here = o_weight.shape[0] // VDIM
    prompts_here = lengths.shape[1]
    q_cols = q_weight.shape[1]
    me = lax.axis_index("narrow")
    mine_first = me == 0

    joined = jnp.concatenate([split_heads(q_weight, heads_here), kva_weight], axis=1)
    joined = lax.all_gather(joined, "wide", axis=0, tiled=True)

    other = swap(tokens)
    whole = jnp.concatenate(
        [jnp.where(mine_first, tokens, other), jnp.where(mine_first, other, tokens)], axis=1
    )

    slots_here = adapter_down.shape[1] // RANK
    prompt_ids = adapter_ids[0]
    id_hot = (prompt_ids[:, None] == jnp.arange(adapter_slot.shape[0])[None, :]).astype(jnp.int32)
    prompt_slot = jnp.sum(id_hot * adapter_slot[None, :], axis=1)
    owner = prompt_slot // slots_here
    local_slot = prompt_slot % slots_here
    picked = jnp.concatenate(
        [
            lax.dynamic_slice_in_dim(adapter_down, local_slot[p] * RANK, RANK, 1)
            for p in range(prompts_here)
        ],
        axis=1,
    )
    picked_other = swap(picked)
    own_block = jnp.repeat(owner == me, RANK)
    chosen = jnp.where(own_block[None, :], picked, picked_other)

    normed = rms_scale(whole.astype(jnp.float32), attn_gain).astype(jnp.bfloat16)
    local_pos = jnp.arange(rows)
    prompt, position, adapter, slot = token_tables(
        lengths[0], adapter_ids[0], adapter_slot, local_pos
    )
    member = (prompt[:, None] == jnp.arange(prompts_here)[None, :]).astype(jnp.float32)
    low = jnp.dot(normed, chosen, preferred_element_type=jnp.float32).reshape(
        rows, prompts_here, RANK
    )
    lowrank = jnp.sum(low * member[:, :, None], axis=1).astype(jnp.bfloat16)
    up_blocks = [
        lax.dynamic_slice_in_dim(adapter_up_weight, prompt_ids[prompt_index] * RANK, RANK, 0)
        for prompt_index in range(prompts_here)
    ]
    up_weight_rows = split_heads(jnp.concatenate(up_blocks, axis=0), heads_here)
    spread_rows = (member.astype(jnp.bfloat16)[:, :, None] * lowrank[:, None, :]).reshape(
        rows, prompts_here * RANK
    )
    half = ROPE // 2
    freqs = jnp.exp(-jnp.log(THETA) * 2.0 * jnp.arange(half).astype(jnp.float32) / (2 * half))
    angle = position.astype(jnp.float32)[:, None] * freqs[None, :]
    cosine = jnp.tile(jnp.cos(angle), (1, heads_here))
    sine = jnp.tile(jnp.sin(angle), (1, heads_here))
    q_nope, q_rope, latent_cache, expanded = project(
        normed, joined, spread_rows, up_weight_rows, cosine, sine, kv_gain, kvb_weight, heads_here
    )
    key_start = (local_pos - position).astype(jnp.int32)
    theirs, mine = attend(
        me.astype(jnp.int32).reshape(1), q_nope, q_rope, expanded, latent_cache,
        key_start, o_weight,
    )
    received = swap(theirs)
    projected = mine.astype(jnp.float32) + received.astype(jnp.float32)
    hidden = (tokens.astype(jnp.float32) + projected).astype(jnp.bfloat16)
    return (hidden, latent_cache)


def solution(mesh):
    return jax.shard_map(
        body,
        mesh=mesh,
        in_specs=(
            P("wide", "narrow"),
            P(),
            P("wide", "narrow"),
            P("wide", None),
            P(),
            P(None, "narrow"),
            P("narrow", None),
            P(None, "narrow"),
            P(None, "narrow"),
            P("wide", None),
            P("wide", None),
            P(),
        ),
        out_specs=(P("wide", "narrow"), P("wide", None)),
        check_vma=False,
    )
```

```python
import jax
import jax.numpy as jnp
from jax import lax
from jax.sharding import PartitionSpec as P
from jax.experimental import pallas as pl
from jax.experimental.pallas import tpu as pltpu

NOPE = 128
ROPE = 64
VDIM = 128
LATENT = 512
RANK = 16
LMAX = 512
QBLOCK = 256
WINDOW = QBLOCK + LMAX
PBLOCK = 256


EPS = 1e-06
THETA = 50000.0
ADAPTER_SCALE = 2.0


def rms_scale(values, gain):
    mean_sq = jnp.mean(values * values, axis=-1, keepdims=True)
    return values * lax.rsqrt(mean_sq + EPS) * gain.astype(jnp.float32)


def rotate(values, positions):
    half = values.shape[-1] // 2
    freqs = jnp.exp(-jnp.log(THETA) * 2.0 * jnp.arange(half).astype(jnp.float32) / (2 * half))
    angle = positions.astype(jnp.float32)[:, None] * freqs[None, :]
    cosine = jnp.cos(angle)
    sine = jnp.sin(angle)
    if values.ndim == 3:
        cosine = cosine[:, None, :]
        sine = sine[:, None, :]
    first = values[..., :half]
    second = values[..., half:]
    return jnp.concatenate(
        [first * cosine - second * sine, first * sine + second * cosine], axis=-1
    )


def token_tables(length_row, id_row, adapter_slot, local_pos):
    ends = jnp.cumsum(length_row)
    starts = ends - length_row
    prompt = jnp.sum((ends[None, :] <= local_pos[:, None]).astype(jnp.int32), axis=1)
    onehot = (prompt[:, None] == jnp.arange(length_row.shape[0])[None, :]).astype(jnp.int32)
    position = local_pos - jnp.sum(onehot * starts[None, :], axis=1)
    adapter = jnp.sum(onehot * id_row[None, :], axis=1)
    slot_hot = (adapter[:, None] == jnp.arange(adapter_slot.shape[0])[None, :]).astype(jnp.int32)
    slot = jnp.sum(slot_hot * adapter_slot[None, :], axis=1)
    return (prompt, position, adapter, slot)


def project_kernel(x_ref, w_ref, sp_ref, up_ref, cos_ref, sin_ref, gain_ref, kvb_ref,
                   qn_ref, qr_ref, cache_ref, kv_ref):
    x = x_ref[...]
    sp = sp_ref[...]
    nope = qn_ref.shape[1]
    heads = qr_ref.shape[0]
    half = heads * ROPE // 2

    def query_part(lo, hi):
        base = jnp.dot(x, w_ref[:, lo:hi], preferred_element_type=jnp.float32)
        return base + ADAPTER_SCALE * jnp.dot(sp, up_ref[:, lo:hi], preferred_element_type=jnp.float32)

    qn_ref[...] = query_part(0, nope).astype(qn_ref.dtype)
    first = query_part(nope, nope + half)
    second = query_part(nope + half, nope + 2 * half)
    cosine = cos_ref[...]
    sine = sin_ref[...]
    turned_first = (first * cosine - second * sine).astype(qr_ref.dtype)
    turned_second = (first * sine + second * cosine).astype(qr_ref.dtype)
    width = ROPE // 2
    for h in range(heads):
        qr_ref[h, :, :width] = turned_first[:, h * width:(h + 1) * width]
        qr_ref[h, :, width:] = turned_second[:, h * width:(h + 1) * width]
    q_end = nope + 2 * half
    pre = jnp.dot(x, w_ref[:, q_end:q_end + LATENT], preferred_element_type=jnp.float32)
    mean_sq = jnp.mean(pre * pre, axis=-1, keepdims=True)
    latent = (pre * lax.rsqrt(mean_sq + EPS) * gain_ref[...]).astype(jnp.bfloat16)
    cache_ref[:, :LATENT] = latent
    key = jnp.dot(x, w_ref[:, q_end + LATENT:], preferred_element_type=jnp.float32)
    key_first = key[:, :ROPE // 2]
    key_second = key[:, ROPE // 2:]
    cosine = cosine[:, :ROPE // 2]
    sine = sine[:, :ROPE // 2]
    cache_ref[:, LATENT:LATENT + ROPE // 2] = (key_first * cosine - key_second * sine).astype(cache_ref.dtype)
    cache_ref[:, LATENT + ROPE // 2:] = (key_first * sine + key_second * cosine).astype(cache_ref.dtype)
    kv_ref[...] = jnp.dot(latent, kvb_ref[...], preferred_element_type=jnp.float32).astype(kv_ref.dtype)


def project(normed, joined, spread, up_rows, cosine, sine, kv_gain, kvb_weight, heads):
    rows, width = normed.shape
    cols = joined.shape[1]
    half = heads * ROPE // 2
    nope = heads * NOPE
    full = lambda shape: pl.BlockSpec(shape, lambda i: (0, 0))
    part = lambda c: pl.BlockSpec((PBLOCK, c), lambda i: (i, 0))
    return pl.pallas_call(
        project_kernel,
        grid=(rows // PBLOCK,),
        in_specs=[
            part(width), full((width, cols)), part(spread.shape[1]), full(up_rows.shape),
            part(half), part(half), full((1, LATENT)), full(kvb_weight.shape),
        ],
        out_specs=[
            part(nope),
            pl.BlockSpec((heads, PBLOCK, ROPE), lambda i: (0, i, 0)),
            part(LATENT + ROPE),
            part(kvb_weight.shape[1]),
        ],
        out_shape=[
            jax.ShapeDtypeStruct((rows, nope), jnp.bfloat16),
            jax.ShapeDtypeStruct((heads, rows, ROPE), jnp.bfloat16),
            jax.ShapeDtypeStruct((rows, LATENT + ROPE), jnp.bfloat16),
            jax.ShapeDtypeStruct((rows, kvb_weight.shape[1]), jnp.bfloat16),
        ],
    )(normed, joined, spread, up_rows, cosine, sine, kv_gain.astype(jnp.float32)[None, :], kvb_weight)


def attention_kernel(me_ref, first_ref, q_nope_ref, qr_ref, kv_ref, cache_ref, kst_ref, wt_ref,
                     wm_ref, theirs_ref, mine_ref, att_ref):
    i = pl.program_id(0)
    heads = qr_ref.shape[0]
    scale = 1.0 / jnp.sqrt(jnp.float32(NOPE + ROPE))
    kst = kst_ref[...]

    def run(start, width):
        start = pl.multiple_of(start, 128)
        row = i * QBLOCK + lax.broadcasted_iota(jnp.int32, (QBLOCK, width), 0)
        col = start + lax.broadcasted_iota(jnp.int32, (QBLOCK, width), 1)
        allowed = (col >= kst) & (col <= row)
        kr = cache_ref[pl.ds(start, width), LATENT:LATENT + ROPE]
        for h in range(heads):
            qn = q_nope_ref[:, h * NOPE:(h + 1) * NOPE]
            qr = qr_ref[h]
            kn = kv_ref[pl.ds(start, width), h * (NOPE + VDIM):h * (NOPE + VDIM) + NOPE]
            s = lax.dot_general(qn, kn, (((1,), (1,)), ((), ())), preferred_element_type=jnp.float32)
            rope = lax.dot_general(qr, kr, (((1,), (1,)), ((), ())), preferred_element_type=jnp.float32)
            s = jnp.where(allowed, (s + rope) * scale, jnp.float32(-1e30))
            top = jnp.max(s, axis=1, keepdims=True)
            e = jnp.exp(s - top)
            w = (e * (1.0 / jnp.sum(e, axis=1, keepdims=True))).astype(jnp.bfloat16)
            v = kv_ref[pl.ds(start, width), h * (NOPE + VDIM) + NOPE:(h + 1) * (NOPE + VDIM)]
            att_ref[:, h * VDIM:(h + 1) * VDIM] = jnp.dot(
                w, v, preferred_element_type=jnp.float32
            ).astype(att_ref.dtype)

    first = first_ref[i]
    one = first >= i * QBLOCK
    two = jnp.logical_and(jnp.logical_not(one), first >= i * QBLOCK - QBLOCK)

    @pl.when(one)
    def _():
        run(i * QBLOCK, QBLOCK)

    @pl.when(two)
    def _():
        run(jnp.maximum(i * QBLOCK - QBLOCK, 0), 2 * QBLOCK)

    @pl.when(jnp.logical_not(jnp.logical_or(one, two)))
    def _():
        run(jnp.maximum(i * QBLOCK - LMAX, 0), WINDOW)

    att = att_ref[...]
    theirs_ref[...] = jnp.dot(att, wt_ref[...], preferred_element_type=jnp.float32).astype(theirs_ref.dtype)
    mine_ref[...] = jnp.dot(att, wm_ref[...], preferred_element_type=jnp.float32).astype(mine_ref.dtype)


def attend(me, q_nope, q_rope, kv, latent_cache, key_start, o_weight):
    rows = q_nope.shape[0]
    heads = q_nope.shape[1] // NOPE
    out_half = o_weight.shape[1] // 2
    grid_spec = pltpu.PrefetchScalarGridSpec(
        num_scalar_prefetch=2,
        grid=(rows // QBLOCK,),
        in_specs=[
            pl.BlockSpec((QBLOCK, heads * NOPE), lambda i, m, f: (i, 0)),
            pl.BlockSpec((heads, QBLOCK, ROPE), lambda i, m, f: (0, i, 0)),
            pl.BlockSpec((rows, heads * (NOPE + VDIM)), lambda i, m, f: (0, 0)),
            pl.BlockSpec((rows, LATENT + ROPE), lambda i, m, f: (0, 0)),
            pl.BlockSpec((QBLOCK, 1), lambda i, m, f: (i, 0)),
            pl.BlockSpec((heads * VDIM, out_half), lambda i, m, f: (0, 1 - m[0])),
            pl.BlockSpec((heads * VDIM, out_half), lambda i, m, f: (0, m[0])),
        ],
        out_specs=[
            pl.BlockSpec((QBLOCK, out_half), lambda i, m, f: (i, 0)),
            pl.BlockSpec((QBLOCK, out_half), lambda i, m, f: (i, 0)),
        ],
        scratch_shapes=[pltpu.VMEM((QBLOCK, heads * VDIM), jnp.bfloat16)],
    )
    return pl.pallas_call(
        attention_kernel,
        grid_spec=grid_spec,
        out_shape=[
            jax.ShapeDtypeStruct((rows, out_half), jnp.bfloat16),
            jax.ShapeDtypeStruct((rows, out_half), jnp.bfloat16),
        ],
    )(me, key_start[::QBLOCK], q_nope, q_rope, kv, latent_cache, key_start[:, None], o_weight, o_weight)


def finish_kernel(tok_ref, mine_ref, rec_ref, out_ref):
    projected = mine_ref[...].astype(jnp.float32) + rec_ref[...].astype(jnp.float32)
    out_ref[...] = (tok_ref[...].astype(jnp.float32) + projected).astype(out_ref.dtype)


def finish(tokens, mine, received):
    rows, cols = tokens.shape
    spec = pl.BlockSpec((QBLOCK, cols), lambda i: (i, 0))
    return pl.pallas_call(
        finish_kernel,
        grid=(rows // QBLOCK,),
        in_specs=[spec, spec, spec],
        out_specs=spec,
        out_shape=jax.ShapeDtypeStruct((rows, cols), tokens.dtype),
    )(tokens, mine, received)


def split_heads(weight, heads):
    parts = weight.reshape(weight.shape[0], heads, NOPE + ROPE)
    half = ROPE // 2
    return jnp.concatenate(
        [
            parts[..., :NOPE].reshape(weight.shape[0], heads * NOPE),
            parts[..., NOPE:NOPE + half].reshape(weight.shape[0], heads * half),
            parts[..., NOPE + half:].reshape(weight.shape[0], heads * half),
        ],
        axis=1,
    )


def swap(values):
    return lax.ppermute(values, "narrow", perm=[(0, 1), (1, 0)])


def body(
    tokens,
    attn_gain,
    q_weight,
    kva_weight,
    kv_gain,
    kvb_weight,
    o_weight,
    adapter_down,
    adapter_up_weight,
    lengths,
    adapter_ids,
    adapter_slot,
):
    rows = tokens.shape[0]
    half_width = tokens.shape[1]
    heads_here = o_weight.shape[0] // VDIM
    prompts_here = lengths.shape[1]
    q_cols = q_weight.shape[1]
    me = lax.axis_index("narrow")
    mine_first = me == 0

    joined = jnp.concatenate([split_heads(q_weight, heads_here), kva_weight], axis=1)
    joined = lax.all_gather(joined, "wide", axis=0, tiled=True)

    other = swap(tokens)
    whole = jnp.concatenate(
        [jnp.where(mine_first, tokens, other), jnp.where(mine_first, other, tokens)], axis=1
    )

    slots_here = adapter_down.shape[1] // RANK
    prompt_ids = adapter_ids[0]
    id_hot = (prompt_ids[:, None] == jnp.arange(adapter_slot.shape[0])[None, :]).astype(jnp.int32)
    prompt_slot = jnp.sum(id_hot * adapter_slot[None, :], axis=1)
    owner = prompt_slot // slots_here
    local_slot = prompt_slot % slots_here
    picked = jnp.concatenate(
        [
            lax.dynamic_slice_in_dim(adapter_down, local_slot[p] * RANK, RANK, 1)
            for p in range(prompts_here)
        ],
        axis=1,
    )
    picked_other = swap(picked)
    own_block = jnp.repeat(owner == me, RANK)
    chosen = jnp.where(own_block[None, :], picked, picked_other)

    normed = rms_scale(whole.astype(jnp.float32), attn_gain).astype(jnp.bfloat16)
    local_pos = jnp.arange(rows)
    prompt, position, adapter, slot = token_tables(
        lengths[0], adapter_ids[0], adapter_slot, local_pos
    )
    member = (prompt[:, None] == jnp.arange(prompts_here)[None, :]).astype(jnp.float32)
    low = jnp.dot(normed, chosen, preferred_element_type=jnp.float32).reshape(
        rows, prompts_here, RANK
    )
    lowrank = jnp.sum(low * member[:, :, None], axis=1).astype(jnp.bfloat16)
    up_blocks = [
        lax.dynamic_slice_in_dim(adapter_up_weight, prompt_ids[prompt_index] * RANK, RANK, 0)
        for prompt_index in range(prompts_here)
    ]
    up_weight_rows = split_heads(jnp.concatenate(up_blocks, axis=0), heads_here)
    spread_rows = (member.astype(jnp.bfloat16)[:, :, None] * lowrank[:, None, :]).reshape(
        rows, prompts_here * RANK
    )
    half = ROPE // 2
    freqs = jnp.exp(-jnp.log(THETA) * 2.0 * jnp.arange(half).astype(jnp.float32) / (2 * half))
    angle = position.astype(jnp.float32)[:, None] * freqs[None, :]
    cosine = jnp.tile(jnp.cos(angle), (1, heads_here))
    sine = jnp.tile(jnp.sin(angle), (1, heads_here))
    q_nope, q_rope, latent_cache, expanded = project(
        normed, joined, spread_rows, up_weight_rows, cosine, sine, kv_gain, kvb_weight, heads_here
    )
    key_start = (local_pos - position).astype(jnp.int32)
    theirs, mine = attend(
        me.astype(jnp.int32).reshape(1), q_nope, q_rope, expanded, latent_cache,
        key_start, o_weight,
    )
    received = swap(theirs)
    hidden = finish(tokens, mine, received)
    return (hidden, latent_cache)


def solution(mesh):
    return jax.shard_map(
        body,
        mesh=mesh,
        in_specs=(
            P("wide", "narrow"),
            P(),
            P("wide", "narrow"),
            P("wide", None),
            P(),
            P(None, "narrow"),
            P("narrow", None),
            P(None, "narrow"),
            P(None, "narrow"),
            P("wide", None),
            P("wide", None),
            P(),
        ),
        out_specs=(P("wide", "narrow"), P("wide", None)),
        check_vma=False,
    )
```

```python
import jax
import jax.numpy as jnp
from jax import lax
from jax.sharding import PartitionSpec as P
from jax.experimental import pallas as pl
from jax.experimental.pallas import tpu as pltpu

NOPE = 128
ROPE = 64
VDIM = 128
LATENT = 512
RANK = 16
LMAX = 512
QBLOCK = 256
WINDOW = QBLOCK + LMAX
PBLOCK = 256


EPS = 1e-06
THETA = 50000.0
ADAPTER_SCALE = 2.0


def rms_scale(values, gain):
    mean_sq = jnp.mean(values * values, axis=-1, keepdims=True)
    return values * lax.rsqrt(mean_sq + EPS) * gain.astype(jnp.float32)


def rotate(values, positions):
    half = values.shape[-1] // 2
    freqs = jnp.exp(-jnp.log(THETA) * 2.0 * jnp.arange(half).astype(jnp.float32) / (2 * half))
    angle = positions.astype(jnp.float32)[:, None] * freqs[None, :]
    cosine = jnp.cos(angle)
    sine = jnp.sin(angle)
    if values.ndim == 3:
        cosine = cosine[:, None, :]
        sine = sine[:, None, :]
    first = values[..., :half]
    second = values[..., half:]
    return jnp.concatenate(
        [first * cosine - second * sine, first * sine + second * cosine], axis=-1
    )


def token_tables(length_row, id_row, adapter_slot, local_pos):
    ends = jnp.cumsum(length_row)
    starts = ends - length_row
    prompt = jnp.sum((ends[None, :] <= local_pos[:, None]).astype(jnp.int32), axis=1)
    onehot = (prompt[:, None] == jnp.arange(length_row.shape[0])[None, :]).astype(jnp.int32)
    position = local_pos - jnp.sum(onehot * starts[None, :], axis=1)
    adapter = jnp.sum(onehot * id_row[None, :], axis=1)
    slot_hot = (adapter[:, None] == jnp.arange(adapter_slot.shape[0])[None, :]).astype(jnp.int32)
    slot = jnp.sum(slot_hot * adapter_slot[None, :], axis=1)
    return (prompt, position, adapter, slot)


def project_kernel(x_ref, w_ref, sp_ref, up_ref, cos_ref, sin_ref, gain_ref, kvb_ref,
                   qn_ref, qr_ref, cache_ref, kv_ref):
    x = x_ref[...]
    sp = sp_ref[...]
    nope = qn_ref.shape[1]
    heads = qr_ref.shape[0]
    half = heads * ROPE // 2

    def query_part(lo, hi):
        base = jnp.dot(x, w_ref[:, lo:hi], preferred_element_type=jnp.float32)
        return base + ADAPTER_SCALE * jnp.dot(sp, up_ref[:, lo:hi], preferred_element_type=jnp.float32)

    qn_ref[...] = query_part(0, nope).astype(qn_ref.dtype)
    first = query_part(nope, nope + half)
    second = query_part(nope + half, nope + 2 * half)
    cosine = cos_ref[...]
    sine = sin_ref[...]
    turned_first = (first * cosine - second * sine).astype(qr_ref.dtype)
    turned_second = (first * sine + second * cosine).astype(qr_ref.dtype)
    width = ROPE // 2
    for h in range(heads):
        qr_ref[h, :, :width] = turned_first[:, h * width:(h + 1) * width]
        qr_ref[h, :, width:] = turned_second[:, h * width:(h + 1) * width]
    q_end = nope + 2 * half
    pre = jnp.dot(x, w_ref[:, q_end:q_end + LATENT], preferred_element_type=jnp.float32)
    mean_sq = jnp.mean(pre * pre, axis=-1, keepdims=True)
    latent = (pre * lax.rsqrt(mean_sq + EPS) * gain_ref[...]).astype(jnp.bfloat16)
    cache_ref[:, :LATENT] = latent
    key = jnp.dot(x, w_ref[:, q_end + LATENT:], preferred_element_type=jnp.float32)
    key_first = key[:, :ROPE // 2]
    key_second = key[:, ROPE // 2:]
    cosine = cosine[:, :ROPE // 2]
    sine = sine[:, :ROPE // 2]
    cache_ref[:, LATENT:LATENT + ROPE // 2] = (key_first * cosine - key_second * sine).astype(cache_ref.dtype)
    cache_ref[:, LATENT + ROPE // 2:] = (key_first * sine + key_second * cosine).astype(cache_ref.dtype)
    kv_ref[...] = jnp.dot(latent, kvb_ref[...], preferred_element_type=jnp.float32).astype(kv_ref.dtype)


def project(normed, joined, spread, up_rows, cosine, sine, kv_gain, kvb_weight, heads):
    rows, width = normed.shape
    cols = joined.shape[1]
    half = heads * ROPE // 2
    nope = heads * NOPE
    full = lambda shape: pl.BlockSpec(shape, lambda i: (0, 0))
    part = lambda c: pl.BlockSpec((PBLOCK, c), lambda i: (i, 0))
    return pl.pallas_call(
        project_kernel,
        grid=(rows // PBLOCK,),
        in_specs=[
            part(width), full((width, cols)), part(spread.shape[1]), full(up_rows.shape),
            part(half), part(half), full((1, LATENT)), full(kvb_weight.shape),
        ],
        out_specs=[
            part(nope),
            pl.BlockSpec((heads, PBLOCK, ROPE), lambda i: (0, i, 0)),
            part(LATENT + ROPE),
            part(kvb_weight.shape[1]),
        ],
        out_shape=[
            jax.ShapeDtypeStruct((rows, nope), jnp.bfloat16),
            jax.ShapeDtypeStruct((heads, rows, ROPE), jnp.bfloat16),
            jax.ShapeDtypeStruct((rows, LATENT + ROPE), jnp.bfloat16),
            jax.ShapeDtypeStruct((rows, kvb_weight.shape[1]), jnp.bfloat16),
        ],
    )(normed, joined, spread, up_rows, cosine, sine, kv_gain.astype(jnp.float32)[None, :], kvb_weight)


def attention_kernel(me_ref, first_ref, q_nope_ref, qr_ref, kv_ref, cache_ref, kst_ref, wt_ref,
                     wm_ref, theirs_ref, mine_ref, att_ref):
    i = pl.program_id(0)
    heads = qr_ref.shape[0]
    scale = 1.0 / jnp.sqrt(jnp.float32(NOPE + ROPE))
    kst = kst_ref[...]

    def run(start, width):
        start = pl.multiple_of(start, 128)
        row = i * QBLOCK + lax.broadcasted_iota(jnp.int32, (QBLOCK, width), 0)
        col = start + lax.broadcasted_iota(jnp.int32, (QBLOCK, width), 1)
        allowed = (col >= kst) & (col <= row)
        kr = cache_ref[pl.ds(start, width), LATENT:LATENT + ROPE]
        for h in range(heads):
            qn = q_nope_ref[:, h * NOPE:(h + 1) * NOPE]
            qr = qr_ref[h]
            kn = kv_ref[pl.ds(start, width), h * (NOPE + VDIM):h * (NOPE + VDIM) + NOPE]
            s = lax.dot_general(qn, kn, (((1,), (1,)), ((), ())), preferred_element_type=jnp.float32)
            rope = lax.dot_general(qr, kr, (((1,), (1,)), ((), ())), preferred_element_type=jnp.float32)
            s = jnp.where(allowed, (s + rope) * scale, jnp.float32(-1e30))
            top = jnp.max(s, axis=1, keepdims=True)
            e = jnp.exp(s - top)
            w = (e * (1.0 / jnp.sum(e, axis=1, keepdims=True))).astype(jnp.bfloat16)
            v = kv_ref[pl.ds(start, width), h * (NOPE + VDIM) + NOPE:(h + 1) * (NOPE + VDIM)]
            att_ref[:, h * VDIM:(h + 1) * VDIM] = jnp.dot(
                w, v, preferred_element_type=jnp.float32
            ).astype(att_ref.dtype)

    first = first_ref[i]
    steps = LMAX // 128
    extra = jnp.clip((i * QBLOCK - first + 127) // 128, 0, steps)
    for k in range(steps + 1):

        @pl.when(extra == k)
        def _():
            run(jnp.maximum(i * QBLOCK - 128 * k, 0), QBLOCK + 128 * k)

    att = att_ref[...]
    theirs_ref[...] = jnp.dot(att, wt_ref[...], preferred_element_type=jnp.float32).astype(theirs_ref.dtype)
    mine_ref[...] = jnp.dot(att, wm_ref[...], preferred_element_type=jnp.float32).astype(mine_ref.dtype)


def attend(me, q_nope, q_rope, kv, latent_cache, key_start, o_weight):
    rows = q_nope.shape[0]
    heads = q_nope.shape[1] // NOPE
    out_half = o_weight.shape[1] // 2
    grid_spec = pltpu.PrefetchScalarGridSpec(
        num_scalar_prefetch=2,
        grid=(rows // QBLOCK,),
        in_specs=[
            pl.BlockSpec((QBLOCK, heads * NOPE), lambda i, m, f: (i, 0)),
            pl.BlockSpec((heads, QBLOCK, ROPE), lambda i, m, f: (0, i, 0)),
            pl.BlockSpec((rows, heads * (NOPE + VDIM)), lambda i, m, f: (0, 0)),
            pl.BlockSpec((rows, LATENT + ROPE), lambda i, m, f: (0, 0)),
            pl.BlockSpec((QBLOCK, 1), lambda i, m, f: (i, 0)),
            pl.BlockSpec((heads * VDIM, out_half), lambda i, m, f: (0, 1 - m[0])),
            pl.BlockSpec((heads * VDIM, out_half), lambda i, m, f: (0, m[0])),
        ],
        out_specs=[
            pl.BlockSpec((QBLOCK, out_half), lambda i, m, f: (i, 0)),
            pl.BlockSpec((QBLOCK, out_half), lambda i, m, f: (i, 0)),
        ],
        scratch_shapes=[pltpu.VMEM((QBLOCK, heads * VDIM), jnp.bfloat16)],
    )
    return pl.pallas_call(
        attention_kernel,
        grid_spec=grid_spec,
        out_shape=[
            jax.ShapeDtypeStruct((rows, out_half), jnp.bfloat16),
            jax.ShapeDtypeStruct((rows, out_half), jnp.bfloat16),
        ],
    )(me, key_start[::QBLOCK], q_nope, q_rope, kv, latent_cache, key_start[:, None], o_weight, o_weight)


def finish_kernel(tok_ref, mine_ref, rec_ref, out_ref):
    projected = mine_ref[...].astype(jnp.float32) + rec_ref[...].astype(jnp.float32)
    out_ref[...] = (tok_ref[...].astype(jnp.float32) + projected).astype(out_ref.dtype)


def finish(tokens, mine, received):
    rows, cols = tokens.shape
    spec = pl.BlockSpec((QBLOCK, cols), lambda i: (i, 0))
    return pl.pallas_call(
        finish_kernel,
        grid=(rows // QBLOCK,),
        in_specs=[spec, spec, spec],
        out_specs=spec,
        out_shape=jax.ShapeDtypeStruct((rows, cols), tokens.dtype),
    )(tokens, mine, received)


def split_heads(weight, heads):
    parts = weight.reshape(weight.shape[0], heads, NOPE + ROPE)
    half = ROPE // 2
    return jnp.concatenate(
        [
            parts[..., :NOPE].reshape(weight.shape[0], heads * NOPE),
            parts[..., NOPE:NOPE + half].reshape(weight.shape[0], heads * half),
            parts[..., NOPE + half:].reshape(weight.shape[0], heads * half),
        ],
        axis=1,
    )


def swap(values):
    return lax.ppermute(values, "narrow", perm=[(0, 1), (1, 0)])


def body(
    tokens,
    attn_gain,
    q_weight,
    kva_weight,
    kv_gain,
    kvb_weight,
    o_weight,
    adapter_down,
    adapter_up_weight,
    lengths,
    adapter_ids,
    adapter_slot,
):
    rows = tokens.shape[0]
    half_width = tokens.shape[1]
    heads_here = o_weight.shape[0] // VDIM
    prompts_here = lengths.shape[1]
    q_cols = q_weight.shape[1]
    me = lax.axis_index("narrow")
    mine_first = me == 0

    joined = jnp.concatenate([split_heads(q_weight, heads_here), kva_weight], axis=1)
    joined = lax.all_gather(joined, "wide", axis=0, tiled=True)

    other = swap(tokens)
    whole = jnp.concatenate(
        [jnp.where(mine_first, tokens, other), jnp.where(mine_first, other, tokens)], axis=1
    )

    slots_here = adapter_down.shape[1] // RANK
    prompt_ids = adapter_ids[0]
    id_hot = (prompt_ids[:, None] == jnp.arange(adapter_slot.shape[0])[None, :]).astype(jnp.int32)
    prompt_slot = jnp.sum(id_hot * adapter_slot[None, :], axis=1)
    owner = prompt_slot // slots_here
    local_slot = prompt_slot % slots_here
    picked = jnp.concatenate(
        [
            lax.dynamic_slice_in_dim(adapter_down, local_slot[p] * RANK, RANK, 1)
            for p in range(prompts_here)
        ],
        axis=1,
    )
    picked_other = swap(picked)
    own_block = jnp.repeat(owner == me, RANK)
    chosen = jnp.where(own_block[None, :], picked, picked_other)

    normed = rms_scale(whole.astype(jnp.float32), attn_gain).astype(jnp.bfloat16)
    local_pos = jnp.arange(rows)
    prompt, position, adapter, slot = token_tables(
        lengths[0], adapter_ids[0], adapter_slot, local_pos
    )
    member = (prompt[:, None] == jnp.arange(prompts_here)[None, :]).astype(jnp.float32)
    low = jnp.dot(normed, chosen, preferred_element_type=jnp.float32).reshape(
        rows, prompts_here, RANK
    )
    lowrank = jnp.sum(low * member[:, :, None], axis=1).astype(jnp.bfloat16)
    up_blocks = [
        lax.dynamic_slice_in_dim(adapter_up_weight, prompt_ids[prompt_index] * RANK, RANK, 0)
        for prompt_index in range(prompts_here)
    ]
    up_weight_rows = split_heads(jnp.concatenate(up_blocks, axis=0), heads_here)
    spread_rows = (member.astype(jnp.bfloat16)[:, :, None] * lowrank[:, None, :]).reshape(
        rows, prompts_here * RANK
    )
    half = ROPE // 2
    freqs = jnp.exp(-jnp.log(THETA) * 2.0 * jnp.arange(half).astype(jnp.float32) / (2 * half))
    angle = position.astype(jnp.float32)[:, None] * freqs[None, :]
    cosine = jnp.tile(jnp.cos(angle), (1, heads_here))
    sine = jnp.tile(jnp.sin(angle), (1, heads_here))
    q_nope, q_rope, latent_cache, expanded = project(
        normed, joined, spread_rows, up_weight_rows, cosine, sine, kv_gain, kvb_weight, heads_here
    )
    key_start = (local_pos - position).astype(jnp.int32)
    theirs, mine = attend(
        me.astype(jnp.int32).reshape(1), q_nope, q_rope, expanded, latent_cache,
        key_start, o_weight,
    )
    received = swap(theirs)
    hidden = finish(tokens, mine, received)
    return (hidden, latent_cache)


def solution(mesh):
    return jax.shard_map(
        body,
        mesh=mesh,
        in_specs=(
            P("wide", "narrow"),
            P(),
            P("wide", "narrow"),
            P("wide", None),
            P(),
            P(None, "narrow"),
            P("narrow", None),
            P(None, "narrow"),
            P(None, "narrow"),
            P("wide", None),
            P("wide", None),
            P(),
        ),
        out_specs=(P("wide", "narrow"), P("wide", None)),
        check_vma=False,
    )
```

```python
import jax
import jax.numpy as jnp
from jax import lax
from jax.sharding import PartitionSpec as P
from jax.experimental import pallas as pl
from jax.experimental.pallas import tpu as pltpu

NOPE = 128
ROPE = 64
VDIM = 128
LATENT = 512
RANK = 16
LMAX = 512
QBLOCK = 256
WINDOW = QBLOCK + LMAX
PBLOCK = 512


EPS = 1e-06
THETA = 50000.0
ADAPTER_SCALE = 2.0


def rms_scale(values, gain):
    mean_sq = jnp.mean(values * values, axis=-1, keepdims=True)
    return values * lax.rsqrt(mean_sq + EPS) * gain.astype(jnp.float32)


def rotate(values, positions):
    half = values.shape[-1] // 2
    freqs = jnp.exp(-jnp.log(THETA) * 2.0 * jnp.arange(half).astype(jnp.float32) / (2 * half))
    angle = positions.astype(jnp.float32)[:, None] * freqs[None, :]
    cosine = jnp.cos(angle)
    sine = jnp.sin(angle)
    if values.ndim == 3:
        cosine = cosine[:, None, :]
        sine = sine[:, None, :]
    first = values[..., :half]
    second = values[..., half:]
    return jnp.concatenate(
        [first * cosine - second * sine, first * sine + second * cosine], axis=-1
    )


def token_tables(length_row, id_row, adapter_slot, local_pos):
    ends = jnp.cumsum(length_row)
    starts = ends - length_row
    prompt = jnp.sum((ends[None, :] <= local_pos[:, None]).astype(jnp.int32), axis=1)
    onehot = (prompt[:, None] == jnp.arange(length_row.shape[0])[None, :]).astype(jnp.int32)
    position = local_pos - jnp.sum(onehot * starts[None, :], axis=1)
    adapter = jnp.sum(onehot * id_row[None, :], axis=1)
    slot_hot = (adapter[:, None] == jnp.arange(adapter_slot.shape[0])[None, :]).astype(jnp.int32)
    slot = jnp.sum(slot_hot * adapter_slot[None, :], axis=1)
    return (prompt, position, adapter, slot)


def project_kernel(x_ref, w_ref, sp_ref, up_ref, cos_ref, sin_ref, gain_ref, kvb_ref,
                   qn_ref, qr_ref, cache_ref, kv_ref):
    x = x_ref[...]
    sp = sp_ref[...]
    nope = qn_ref.shape[1]
    heads = qr_ref.shape[0]
    half = heads * ROPE // 2

    def query_part(lo, hi):
        base = jnp.dot(x, w_ref[:, lo:hi], preferred_element_type=jnp.float32)
        return base + ADAPTER_SCALE * jnp.dot(sp, up_ref[:, lo:hi], preferred_element_type=jnp.float32)

    qn_ref[...] = query_part(0, nope).astype(qn_ref.dtype)
    first = query_part(nope, nope + half)
    second = query_part(nope + half, nope + 2 * half)
    cosine = cos_ref[...]
    sine = sin_ref[...]
    turned_first = (first * cosine - second * sine).astype(qr_ref.dtype)
    turned_second = (first * sine + second * cosine).astype(qr_ref.dtype)
    width = ROPE // 2
    for h in range(heads):
        qr_ref[h, :, :width] = turned_first[:, h * width:(h + 1) * width]
        qr_ref[h, :, width:] = turned_second[:, h * width:(h + 1) * width]
    q_end = nope + 2 * half
    pre = jnp.dot(x, w_ref[:, q_end:q_end + LATENT], preferred_element_type=jnp.float32)
    mean_sq = jnp.mean(pre * pre, axis=-1, keepdims=True)
    latent = (pre * lax.rsqrt(mean_sq + EPS) * gain_ref[...]).astype(jnp.bfloat16)
    cache_ref[:, :LATENT] = latent
    key = jnp.dot(x, w_ref[:, q_end + LATENT:], preferred_element_type=jnp.float32)
    key_first = key[:, :ROPE // 2]
    key_second = key[:, ROPE // 2:]
    cosine = cosine[:, :ROPE // 2]
    sine = sine[:, :ROPE // 2]
    cache_ref[:, LATENT:LATENT + ROPE // 2] = (key_first * cosine - key_second * sine).astype(cache_ref.dtype)
    cache_ref[:, LATENT + ROPE // 2:] = (key_first * sine + key_second * cosine).astype(cache_ref.dtype)
    kv_ref[...] = jnp.dot(latent, kvb_ref[...], preferred_element_type=jnp.float32).astype(kv_ref.dtype)


def project(normed, joined, spread, up_rows, cosine, sine, kv_gain, kvb_weight, heads):
    rows, width = normed.shape
    cols = joined.shape[1]
    half = heads * ROPE // 2
    nope = heads * NOPE
    full = lambda shape: pl.BlockSpec(shape, lambda i: (0, 0))
    part = lambda c: pl.BlockSpec((PBLOCK, c), lambda i: (i, 0))
    return pl.pallas_call(
        project_kernel,
        grid=(rows // PBLOCK,),
        in_specs=[
            part(width), full((width, cols)), part(spread.shape[1]), full(up_rows.shape),
            part(half), part(half), full((1, LATENT)), full(kvb_weight.shape),
        ],
        out_specs=[
            part(nope),
            pl.BlockSpec((heads, PBLOCK, ROPE), lambda i: (0, i, 0)),
            part(LATENT + ROPE),
            part(kvb_weight.shape[1]),
        ],
        out_shape=[
            jax.ShapeDtypeStruct((rows, nope), jnp.bfloat16),
            jax.ShapeDtypeStruct((heads, rows, ROPE), jnp.bfloat16),
            jax.ShapeDtypeStruct((rows, LATENT + ROPE), jnp.bfloat16),
            jax.ShapeDtypeStruct((rows, kvb_weight.shape[1]), jnp.bfloat16),
        ],
    )(normed, joined, spread, up_rows, cosine, sine, kv_gain.astype(jnp.float32)[None, :], kvb_weight)


def attention_kernel(me_ref, first_ref, q_nope_ref, qr_ref, kv_ref, cache_ref, kst_ref, wt_ref,
                     wm_ref, theirs_ref, mine_ref, att_ref):
    i = pl.program_id(0)
    heads = qr_ref.shape[0]
    scale = 1.0 / jnp.sqrt(jnp.float32(NOPE + ROPE))
    kst = kst_ref[...]

    def run(start, width):
        start = pl.multiple_of(start, 128)
        row = i * QBLOCK + lax.broadcasted_iota(jnp.int32, (QBLOCK, width), 0)
        col = start + lax.broadcasted_iota(jnp.int32, (QBLOCK, width), 1)
        allowed = (col >= kst) & (col <= row)
        kr = cache_ref[pl.ds(start, width), LATENT:LATENT + ROPE]
        for h in range(heads):
            qn = q_nope_ref[:, h * NOPE:(h + 1) * NOPE]
            qr = qr_ref[h]
            kn = kv_ref[pl.ds(start, width), h * (NOPE + VDIM):h * (NOPE + VDIM) + NOPE]
            s = lax.dot_general(qn, kn, (((1,), (1,)), ((), ())), preferred_element_type=jnp.float32)
            rope = lax.dot_general(qr, kr, (((1,), (1,)), ((), ())), preferred_element_type=jnp.float32)
            s = jnp.where(allowed, (s + rope) * scale, jnp.float32(-1e30))
            top = jnp.max(s, axis=1, keepdims=True)
            e = jnp.exp(s - top)
            w = (e * (1.0 / jnp.sum(e, axis=1, keepdims=True))).astype(jnp.bfloat16)
            v = kv_ref[pl.ds(start, width), h * (NOPE + VDIM) + NOPE:(h + 1) * (NOPE + VDIM)]
            att_ref[:, h * VDIM:(h + 1) * VDIM] = jnp.dot(
                w, v, preferred_element_type=jnp.float32
            ).astype(att_ref.dtype)

    first = first_ref[i]
    one = first >= i * QBLOCK
    two = jnp.logical_and(jnp.logical_not(one), first >= i * QBLOCK - QBLOCK)

    @pl.when(one)
    def _():
        run(i * QBLOCK, QBLOCK)

    @pl.when(two)
    def _():
        run(jnp.maximum(i * QBLOCK - QBLOCK, 0), 2 * QBLOCK)

    @pl.when(jnp.logical_not(jnp.logical_or(one, two)))
    def _():
        run(jnp.maximum(i * QBLOCK - LMAX, 0), WINDOW)

    att = att_ref[...]
    theirs_ref[...] = jnp.dot(att, wt_ref[...], preferred_element_type=jnp.float32).astype(theirs_ref.dtype)
    mine_ref[...] = jnp.dot(att, wm_ref[...], preferred_element_type=jnp.float32).astype(mine_ref.dtype)


def attend(me, q_nope, q_rope, kv, latent_cache, key_start, o_weight):
    rows = q_nope.shape[0]
    heads = q_nope.shape[1] // NOPE
    out_half = o_weight.shape[1] // 2
    grid_spec = pltpu.PrefetchScalarGridSpec(
        num_scalar_prefetch=2,
        grid=(rows // QBLOCK,),
        in_specs=[
            pl.BlockSpec((QBLOCK, heads * NOPE), lambda i, m, f: (i, 0)),
            pl.BlockSpec((heads, QBLOCK, ROPE), lambda i, m, f: (0, i, 0)),
            pl.BlockSpec((rows, heads * (NOPE + VDIM)), lambda i, m, f: (0, 0)),
            pl.BlockSpec((rows, LATENT + ROPE), lambda i, m, f: (0, 0)),
            pl.BlockSpec((QBLOCK, 1), lambda i, m, f: (i, 0)),
            pl.BlockSpec((heads * VDIM, out_half), lambda i, m, f: (0, 1 - m[0])),
            pl.BlockSpec((heads * VDIM, out_half), lambda i, m, f: (0, m[0])),
        ],
        out_specs=[
            pl.BlockSpec((QBLOCK, out_half), lambda i, m, f: (i, 0)),
            pl.BlockSpec((QBLOCK, out_half), lambda i, m, f: (i, 0)),
        ],
        scratch_shapes=[pltpu.VMEM((QBLOCK, heads * VDIM), jnp.bfloat16)],
    )
    return pl.pallas_call(
        attention_kernel,
        grid_spec=grid_spec,
        out_shape=[
            jax.ShapeDtypeStruct((rows, out_half), jnp.bfloat16),
            jax.ShapeDtypeStruct((rows, out_half), jnp.bfloat16),
        ],
    )(me, key_start[::QBLOCK], q_nope, q_rope, kv, latent_cache, key_start[:, None], o_weight, o_weight)


def finish_kernel(tok_ref, mine_ref, rec_ref, out_ref):
    projected = mine_ref[...].astype(jnp.float32) + rec_ref[...].astype(jnp.float32)
    out_ref[...] = (tok_ref[...].astype(jnp.float32) + projected).astype(out_ref.dtype)


def finish(tokens, mine, received):
    rows, cols = tokens.shape
    spec = pl.BlockSpec((QBLOCK, cols), lambda i: (i, 0))
    return pl.pallas_call(
        finish_kernel,
        grid=(rows // QBLOCK,),
        in_specs=[spec, spec, spec],
        out_specs=spec,
        out_shape=jax.ShapeDtypeStruct((rows, cols), tokens.dtype),
    )(tokens, mine, received)


def split_heads(weight, heads):
    parts = weight.reshape(weight.shape[0], heads, NOPE + ROPE)
    half = ROPE // 2
    return jnp.concatenate(
        [
            parts[..., :NOPE].reshape(weight.shape[0], heads * NOPE),
            parts[..., NOPE:NOPE + half].reshape(weight.shape[0], heads * half),
            parts[..., NOPE + half:].reshape(weight.shape[0], heads * half),
        ],
        axis=1,
    )


def swap(values):
    return lax.ppermute(values, "narrow", perm=[(0, 1), (1, 0)])


def body(
    tokens,
    attn_gain,
    q_weight,
    kva_weight,
    kv_gain,
    kvb_weight,
    o_weight,
    adapter_down,
    adapter_up_weight,
    lengths,
    adapter_ids,
    adapter_slot,
):
    rows = tokens.shape[0]
    half_width = tokens.shape[1]
    heads_here = o_weight.shape[0] // VDIM
    prompts_here = lengths.shape[1]
    q_cols = q_weight.shape[1]
    me = lax.axis_index("narrow")
    mine_first = me == 0

    joined = jnp.concatenate([split_heads(q_weight, heads_here), kva_weight], axis=1)
    joined = lax.all_gather(joined, "wide", axis=0, tiled=True)

    other = swap(tokens)
    whole = jnp.concatenate(
        [jnp.where(mine_first, tokens, other), jnp.where(mine_first, other, tokens)], axis=1
    )

    slots_here = adapter_down.shape[1] // RANK
    prompt_ids = adapter_ids[0]
    id_hot = (prompt_ids[:, None] == jnp.arange(adapter_slot.shape[0])[None, :]).astype(jnp.int32)
    prompt_slot = jnp.sum(id_hot * adapter_slot[None, :], axis=1)
    owner = prompt_slot // slots_here
    local_slot = prompt_slot % slots_here
    picked = jnp.concatenate(
        [
            lax.dynamic_slice_in_dim(adapter_down, local_slot[p] * RANK, RANK, 1)
            for p in range(prompts_here)
        ],
        axis=1,
    )
    picked_other = swap(picked)
    own_block = jnp.repeat(owner == me, RANK)
    chosen = jnp.where(own_block[None, :], picked, picked_other)

    normed = rms_scale(whole.astype(jnp.float32), attn_gain).astype(jnp.bfloat16)
    local_pos = jnp.arange(rows)
    prompt, position, adapter, slot = token_tables(
        lengths[0], adapter_ids[0], adapter_slot, local_pos
    )
    member = (prompt[:, None] == jnp.arange(prompts_here)[None, :]).astype(jnp.float32)
    low = jnp.dot(normed, chosen, preferred_element_type=jnp.float32).reshape(
        rows, prompts_here, RANK
    )
    lowrank = jnp.sum(low * member[:, :, None], axis=1).astype(jnp.bfloat16)
    up_blocks = [
        lax.dynamic_slice_in_dim(adapter_up_weight, prompt_ids[prompt_index] * RANK, RANK, 0)
        for prompt_index in range(prompts_here)
    ]
    up_weight_rows = split_heads(jnp.concatenate(up_blocks, axis=0), heads_here)
    spread_rows = (member.astype(jnp.bfloat16)[:, :, None] * lowrank[:, None, :]).reshape(
        rows, prompts_here * RANK
    )
    half = ROPE // 2
    freqs = jnp.exp(-jnp.log(THETA) * 2.0 * jnp.arange(half).astype(jnp.float32) / (2 * half))
    angle = position.astype(jnp.float32)[:, None] * freqs[None, :]
    cosine = jnp.tile(jnp.cos(angle), (1, heads_here))
    sine = jnp.tile(jnp.sin(angle), (1, heads_here))
    q_nope, q_rope, latent_cache, expanded = project(
        normed, joined, spread_rows, up_weight_rows, cosine, sine, kv_gain, kvb_weight, heads_here
    )
    key_start = (local_pos - position).astype(jnp.int32)
    theirs, mine = attend(
        me.astype(jnp.int32).reshape(1), q_nope, q_rope, expanded, latent_cache,
        key_start, o_weight,
    )
    received = swap(theirs)
    hidden = finish(tokens, mine, received)
    return (hidden, latent_cache)


def solution(mesh):
    return jax.shard_map(
        body,
        mesh=mesh,
        in_specs=(
            P("wide", "narrow"),
            P(),
            P("wide", "narrow"),
            P("wide", None),
            P(),
            P(None, "narrow"),
            P("narrow", None),
            P(None, "narrow"),
            P(None, "narrow"),
            P("wide", None),
            P("wide", None),
            P(),
        ),
        out_specs=(P("wide", "narrow"), P("wide", None)),
        check_vma=False,
    )
```

```python
import jax
import jax.numpy as jnp
from jax import lax
from jax.sharding import PartitionSpec as P
from jax.experimental import pallas as pl
from jax.experimental.pallas import tpu as pltpu

NOPE = 128
ROPE = 64
VDIM = 128
LATENT = 512
RANK = 16
LMAX = 512
QBLOCK = 256
WINDOW = QBLOCK + LMAX
PBLOCK = 256


EPS = 1e-06
THETA = 50000.0
ADAPTER_SCALE = 2.0


def rms_scale(values, gain):
    mean_sq = jnp.mean(values * values, axis=-1, keepdims=True)
    return values * lax.rsqrt(mean_sq + EPS) * gain.astype(jnp.float32)


def rotate(values, positions):
    half = values.shape[-1] // 2
    freqs = jnp.exp(-jnp.log(THETA) * 2.0 * jnp.arange(half).astype(jnp.float32) / (2 * half))
    angle = positions.astype(jnp.float32)[:, None] * freqs[None, :]
    cosine = jnp.cos(angle)
    sine = jnp.sin(angle)
    if values.ndim == 3:
        cosine = cosine[:, None, :]
        sine = sine[:, None, :]
    first = values[..., :half]
    second = values[..., half:]
    return jnp.concatenate(
        [first * cosine - second * sine, first * sine + second * cosine], axis=-1
    )


def token_tables(length_row, id_row, adapter_slot, local_pos):
    ends = jnp.cumsum(length_row)
    starts = ends - length_row
    prompt = jnp.sum((ends[None, :] <= local_pos[:, None]).astype(jnp.int32), axis=1)
    onehot = (prompt[:, None] == jnp.arange(length_row.shape[0])[None, :]).astype(jnp.int32)
    position = local_pos - jnp.sum(onehot * starts[None, :], axis=1)
    adapter = jnp.sum(onehot * id_row[None, :], axis=1)
    slot_hot = (adapter[:, None] == jnp.arange(adapter_slot.shape[0])[None, :]).astype(jnp.int32)
    slot = jnp.sum(slot_hot * adapter_slot[None, :], axis=1)
    return (prompt, position, adapter, slot)


def project_kernel(x_ref, w_ref, sp_ref, up_ref, cos_ref, sin_ref, gain_ref, kvb_ref,
                   qn_ref, qr_ref, cache_ref, kv_ref):
    x = x_ref[...]
    sp = sp_ref[...]
    nope = qn_ref.shape[1]
    heads = qr_ref.shape[0]
    half = heads * ROPE // 2

    def query_part(lo, hi):
        base = jnp.dot(x, w_ref[:, lo:hi], preferred_element_type=jnp.float32)
        return base + ADAPTER_SCALE * jnp.dot(sp, up_ref[:, lo:hi], preferred_element_type=jnp.float32)

    qn_ref[...] = query_part(0, nope).astype(qn_ref.dtype)
    first = query_part(nope, nope + half)
    second = query_part(nope + half, nope + 2 * half)
    cosine = cos_ref[...]
    sine = sin_ref[...]
    turned_first = (first * cosine - second * sine).astype(qr_ref.dtype)
    turned_second = (first * sine + second * cosine).astype(qr_ref.dtype)
    width = ROPE // 2
    for h in range(heads):
        qr_ref[h, :, :width] = turned_first[:, h * width:(h + 1) * width]
        qr_ref[h, :, width:] = turned_second[:, h * width:(h + 1) * width]
    q_end = nope + 2 * half
    pre = jnp.dot(x, w_ref[:, q_end:q_end + LATENT], preferred_element_type=jnp.float32)
    mean_sq = jnp.mean(pre * pre, axis=-1, keepdims=True)
    latent = (pre * lax.rsqrt(mean_sq + EPS) * gain_ref[...]).astype(jnp.bfloat16)
    cache_ref[:, :LATENT] = latent
    key = jnp.dot(x, w_ref[:, q_end + LATENT:], preferred_element_type=jnp.float32)
    key_first = key[:, :ROPE // 2]
    key_second = key[:, ROPE // 2:]
    cosine = cosine[:, :ROPE // 2]
    sine = sine[:, :ROPE // 2]
    cache_ref[:, LATENT:LATENT + ROPE // 2] = (key_first * cosine - key_second * sine).astype(cache_ref.dtype)
    cache_ref[:, LATENT + ROPE // 2:] = (key_first * sine + key_second * cosine).astype(cache_ref.dtype)
    kv_ref[...] = jnp.dot(latent, kvb_ref[...], preferred_element_type=jnp.float32).astype(kv_ref.dtype)


def project(normed, joined, spread, up_rows, cosine, sine, kv_gain, kvb_weight, heads):
    rows, width = normed.shape
    cols = joined.shape[1]
    half = heads * ROPE // 2
    nope = heads * NOPE
    full = lambda shape: pl.BlockSpec(shape, lambda i: (0, 0))
    part = lambda c: pl.BlockSpec((PBLOCK, c), lambda i: (i, 0))
    return pl.pallas_call(
        project_kernel,
        grid=(rows // PBLOCK,),
        in_specs=[
            part(width), full((width, cols)), part(spread.shape[1]), full(up_rows.shape),
            part(half), part(half), full((1, LATENT)), full(kvb_weight.shape),
        ],
        out_specs=[
            part(nope),
            pl.BlockSpec((heads, PBLOCK, ROPE), lambda i: (0, i, 0)),
            part(LATENT + ROPE),
            part(kvb_weight.shape[1]),
        ],
        out_shape=[
            jax.ShapeDtypeStruct((rows, nope), jnp.bfloat16),
            jax.ShapeDtypeStruct((heads, rows, ROPE), jnp.bfloat16),
            jax.ShapeDtypeStruct((rows, LATENT + ROPE), jnp.bfloat16),
            jax.ShapeDtypeStruct((rows, kvb_weight.shape[1]), jnp.bfloat16),
        ],
    )(normed, joined, spread, up_rows, cosine, sine, kv_gain.astype(jnp.float32)[None, :], kvb_weight)


def attention_kernel(me_ref, first_ref, q_nope_ref, qr_ref, kv_ref, cache_ref, kst_ref, wt_ref,
                     wm_ref, theirs_ref, mine_ref, att_ref):
    i = pl.program_id(0)
    heads = qr_ref.shape[0]
    scale = 1.0 / jnp.sqrt(jnp.float32(NOPE + ROPE))
    kst = kst_ref[...]

    def run(start, width):
        start = pl.multiple_of(start, 128)
        row = i * QBLOCK + lax.broadcasted_iota(jnp.int32, (QBLOCK, width), 0)
        col = start + lax.broadcasted_iota(jnp.int32, (QBLOCK, width), 1)
        allowed = (col >= kst) & (col <= row)
        kr = cache_ref[pl.ds(start, width), LATENT:LATENT + ROPE]
        for h in range(heads):
            qn = q_nope_ref[:, h * NOPE:(h + 1) * NOPE]
            qr = qr_ref[h]
            kn = kv_ref[pl.ds(start, width), h * (NOPE + VDIM):h * (NOPE + VDIM) + NOPE]
            s = lax.dot_general(qn, kn, (((1,), (1,)), ((), ())), preferred_element_type=jnp.float32)
            rope = lax.dot_general(qr, kr, (((1,), (1,)), ((), ())), preferred_element_type=jnp.float32)
            s = jnp.where(allowed, (s + rope) * scale, jnp.float32(-1e30))
            top = jnp.max(s, axis=1, keepdims=True)
            e = jnp.exp(s - top)
            w = (e * (1.0 / jnp.sum(e, axis=1, keepdims=True))).astype(jnp.bfloat16)
            v = kv_ref[pl.ds(start, width), h * (NOPE + VDIM) + NOPE:(h + 1) * (NOPE + VDIM)]
            att_ref[:, h * VDIM:(h + 1) * VDIM] = jnp.dot(
                w, v, preferred_element_type=jnp.float32
            ).astype(att_ref.dtype)

    first = first_ref[i]
    one = first >= i * QBLOCK
    two = jnp.logical_and(jnp.logical_not(one), first >= i * QBLOCK - QBLOCK)

    @pl.when(one)
    def _():
        run(i * QBLOCK, QBLOCK)

    @pl.when(two)
    def _():
        run(jnp.maximum(i * QBLOCK - QBLOCK, 0), 2 * QBLOCK)

    @pl.when(jnp.logical_not(jnp.logical_or(one, two)))
    def _():
        run(jnp.maximum(i * QBLOCK - LMAX, 0), WINDOW)

    att = att_ref[...]
    theirs_ref[...] = jnp.dot(att, wt_ref[...], preferred_element_type=jnp.float32).astype(theirs_ref.dtype)
    mine_ref[...] = jnp.dot(att, wm_ref[...], preferred_element_type=jnp.float32).astype(mine_ref.dtype)


def attend(me, q_nope, q_rope, kv, latent_cache, key_start, o_weight):
    rows = q_nope.shape[0]
    heads = q_nope.shape[1] // NOPE
    out_half = o_weight.shape[1] // 2
    grid_spec = pltpu.PrefetchScalarGridSpec(
        num_scalar_prefetch=2,
        grid=(rows // QBLOCK,),
        in_specs=[
            pl.BlockSpec((QBLOCK, heads * NOPE), lambda i, m, f: (i, 0)),
            pl.BlockSpec((heads, QBLOCK, ROPE), lambda i, m, f: (0, i, 0)),
            pl.BlockSpec((rows, heads * (NOPE + VDIM)), lambda i, m, f: (0, 0)),
            pl.BlockSpec((rows, LATENT + ROPE), lambda i, m, f: (0, 0)),
            pl.BlockSpec((QBLOCK, 1), lambda i, m, f: (i, 0)),
            pl.BlockSpec((heads * VDIM, out_half), lambda i, m, f: (0, 1 - m[0])),
            pl.BlockSpec((heads * VDIM, out_half), lambda i, m, f: (0, m[0])),
        ],
        out_specs=[
            pl.BlockSpec((QBLOCK, out_half), lambda i, m, f: (i, 0)),
            pl.BlockSpec((QBLOCK, out_half), lambda i, m, f: (i, 0)),
        ],
        scratch_shapes=[pltpu.VMEM((QBLOCK, heads * VDIM), jnp.bfloat16)],
    )
    return pl.pallas_call(
        attention_kernel,
        grid_spec=grid_spec,
        out_shape=[
            jax.ShapeDtypeStruct((rows, out_half), jnp.bfloat16),
            jax.ShapeDtypeStruct((rows, out_half), jnp.bfloat16),
        ],
    )(me, key_start[::QBLOCK], q_nope, q_rope, kv, latent_cache, key_start[:, None], o_weight, o_weight)


def finish_kernel(tok_ref, mine_ref, rec_ref, out_ref):
    projected = mine_ref[...].astype(jnp.float32) + rec_ref[...].astype(jnp.float32)
    out_ref[...] = (tok_ref[...].astype(jnp.float32) + projected).astype(out_ref.dtype)


def finish(tokens, mine, received):
    rows, cols = tokens.shape
    block = 128
    spec = pl.BlockSpec((block, cols), lambda i: (i, 0))
    return pl.pallas_call(
        finish_kernel,
        grid=(rows // block,),
        in_specs=[spec, spec, spec],
        out_specs=spec,
        out_shape=jax.ShapeDtypeStruct((rows, cols), tokens.dtype),
    )(tokens, mine, received)


def split_heads(weight, heads):
    parts = weight.reshape(weight.shape[0], heads, NOPE + ROPE)
    half = ROPE // 2
    return jnp.concatenate(
        [
            parts[..., :NOPE].reshape(weight.shape[0], heads * NOPE),
            parts[..., NOPE:NOPE + half].reshape(weight.shape[0], heads * half),
            parts[..., NOPE + half:].reshape(weight.shape[0], heads * half),
        ],
        axis=1,
    )


def swap(values):
    return lax.ppermute(values, "narrow", perm=[(0, 1), (1, 0)])


def body(
    tokens,
    attn_gain,
    q_weight,
    kva_weight,
    kv_gain,
    kvb_weight,
    o_weight,
    adapter_down,
    adapter_up_weight,
    lengths,
    adapter_ids,
    adapter_slot,
):
    rows = tokens.shape[0]
    half_width = tokens.shape[1]
    heads_here = o_weight.shape[0] // VDIM
    prompts_here = lengths.shape[1]
    q_cols = q_weight.shape[1]
    me = lax.axis_index("narrow")
    mine_first = me == 0

    joined = jnp.concatenate([split_heads(q_weight, heads_here), kva_weight], axis=1)
    joined = lax.all_gather(joined, "wide", axis=0, tiled=True)

    other = swap(tokens)
    whole = jnp.concatenate(
        [jnp.where(mine_first, tokens, other), jnp.where(mine_first, other, tokens)], axis=1
    )

    slots_here = adapter_down.shape[1] // RANK
    prompt_ids = adapter_ids[0]
    id_hot = (prompt_ids[:, None] == jnp.arange(adapter_slot.shape[0])[None, :]).astype(jnp.int32)
    prompt_slot = jnp.sum(id_hot * adapter_slot[None, :], axis=1)
    owner = prompt_slot // slots_here
    local_slot = prompt_slot % slots_here
    picked = jnp.concatenate(
        [
            lax.dynamic_slice_in_dim(adapter_down, local_slot[p] * RANK, RANK, 1)
            for p in range(prompts_here)
        ],
        axis=1,
    )
    picked_other = swap(picked)
    own_block = jnp.repeat(owner == me, RANK)
    chosen = jnp.where(own_block[None, :], picked, picked_other)

    normed = rms_scale(whole.astype(jnp.float32), attn_gain).astype(jnp.bfloat16)
    local_pos = jnp.arange(rows)
    prompt, position, adapter, slot = token_tables(
        lengths[0], adapter_ids[0], adapter_slot, local_pos
    )
    member = (prompt[:, None] == jnp.arange(prompts_here)[None, :]).astype(jnp.float32)
    low = jnp.dot(normed, chosen, preferred_element_type=jnp.float32).reshape(
        rows, prompts_here, RANK
    )
    lowrank = jnp.sum(low * member[:, :, None], axis=1).astype(jnp.bfloat16)
    up_blocks = [
        lax.dynamic_slice_in_dim(adapter_up_weight, prompt_ids[prompt_index] * RANK, RANK, 0)
        for prompt_index in range(prompts_here)
    ]
    up_weight_rows = split_heads(jnp.concatenate(up_blocks, axis=0), heads_here)
    spread_rows = (member.astype(jnp.bfloat16)[:, :, None] * lowrank[:, None, :]).reshape(
        rows, prompts_here * RANK
    )
    half = ROPE // 2
    freqs = jnp.exp(-jnp.log(THETA) * 2.0 * jnp.arange(half).astype(jnp.float32) / (2 * half))
    angle = position.astype(jnp.float32)[:, None] * freqs[None, :]
    cosine = jnp.tile(jnp.cos(angle), (1, heads_here))
    sine = jnp.tile(jnp.sin(angle), (1, heads_here))
    q_nope, q_rope, latent_cache, expanded = project(
        normed, joined, spread_rows, up_weight_rows, cosine, sine, kv_gain, kvb_weight, heads_here
    )
    key_start = (local_pos - position).astype(jnp.int32)
    theirs, mine = attend(
        me.astype(jnp.int32).reshape(1), q_nope, q_rope, expanded, latent_cache,
        key_start, o_weight,
    )
    received = swap(theirs)
    hidden = finish(tokens, mine, received)
    return (hidden, latent_cache)


def solution(mesh):
    return jax.shard_map(
        body,
        mesh=mesh,
        in_specs=(
            P("wide", "narrow"),
            P(),
            P("wide", "narrow"),
            P("wide", None),
            P(),
            P(None, "narrow"),
            P("narrow", None),
            P(None, "narrow"),
            P(None, "narrow"),
            P("wide", None),
            P("wide", None),
            P(),
        ),
        out_specs=(P("wide", "narrow"), P("wide", None)),
        check_vma=False,
    )
```

```python
import jax
import jax.numpy as jnp
from jax import lax
from jax.sharding import PartitionSpec as P
from jax.experimental import pallas as pl
from jax.experimental.pallas import tpu as pltpu

NOPE = 128
ROPE = 64
VDIM = 128
LATENT = 512
RANK = 16
LMAX = 512
QBLOCK = 256
WINDOW = QBLOCK + LMAX
PBLOCK = 256


EPS = 1e-06
THETA = 50000.0
ADAPTER_SCALE = 2.0


def rms_scale(values, gain):
    mean_sq = jnp.mean(values * values, axis=-1, keepdims=True)
    return values * lax.rsqrt(mean_sq + EPS) * gain.astype(jnp.float32)


def rotate(values, positions):
    half = values.shape[-1] // 2
    freqs = jnp.exp(-jnp.log(THETA) * 2.0 * jnp.arange(half).astype(jnp.float32) / (2 * half))
    angle = positions.astype(jnp.float32)[:, None] * freqs[None, :]
    cosine = jnp.cos(angle)
    sine = jnp.sin(angle)
    if values.ndim == 3:
        cosine = cosine[:, None, :]
        sine = sine[:, None, :]
    first = values[..., :half]
    second = values[..., half:]
    return jnp.concatenate(
        [first * cosine - second * sine, first * sine + second * cosine], axis=-1
    )


def token_tables(length_row, id_row, adapter_slot, local_pos):
    ends = jnp.cumsum(length_row)
    starts = ends - length_row
    prompt = jnp.sum((ends[None, :] <= local_pos[:, None]).astype(jnp.int32), axis=1)
    onehot = (prompt[:, None] == jnp.arange(length_row.shape[0])[None, :]).astype(jnp.int32)
    position = local_pos - jnp.sum(onehot * starts[None, :], axis=1)
    adapter = jnp.sum(onehot * id_row[None, :], axis=1)
    slot_hot = (adapter[:, None] == jnp.arange(adapter_slot.shape[0])[None, :]).astype(jnp.int32)
    slot = jnp.sum(slot_hot * adapter_slot[None, :], axis=1)
    return (prompt, position, adapter, slot)


def project_kernel(x_ref, w_ref, sp_ref, up_ref, cos_ref, sin_ref, gain_ref, kvb_ref,
                   qn_ref, qr_ref, cache_ref, kv_ref):
    x = x_ref[...]
    sp = sp_ref[...]
    nope = qn_ref.shape[1]
    heads = qr_ref.shape[0]
    half = heads * ROPE // 2

    def query_part(lo, hi):
        base = jnp.dot(x, w_ref[:, lo:hi], preferred_element_type=jnp.float32)
        return base + ADAPTER_SCALE * jnp.dot(sp, up_ref[:, lo:hi], preferred_element_type=jnp.float32)

    qn_ref[...] = query_part(0, nope).astype(qn_ref.dtype)
    first = query_part(nope, nope + half)
    second = query_part(nope + half, nope + 2 * half)
    cosine = cos_ref[...]
    sine = sin_ref[...]
    turned_first = (first * cosine - second * sine).astype(qr_ref.dtype)
    turned_second = (first * sine + second * cosine).astype(qr_ref.dtype)
    width = ROPE // 2
    for h in range(heads):
        qr_ref[h, :, :width] = turned_first[:, h * width:(h + 1) * width]
        qr_ref[h, :, width:] = turned_second[:, h * width:(h + 1) * width]
    q_end = nope + 2 * half
    pre = jnp.dot(x, w_ref[:, q_end:q_end + LATENT], preferred_element_type=jnp.float32)
    mean_sq = jnp.mean(pre * pre, axis=-1, keepdims=True)
    latent = (pre * lax.rsqrt(mean_sq + EPS) * gain_ref[...]).astype(jnp.bfloat16)
    cache_ref[:, :LATENT] = latent
    key = jnp.dot(x, w_ref[:, q_end + LATENT:], preferred_element_type=jnp.float32)
    key_first = key[:, :ROPE // 2]
    key_second = key[:, ROPE // 2:]
    cosine = cosine[:, :ROPE // 2]
    sine = sine[:, :ROPE // 2]
    cache_ref[:, LATENT:LATENT + ROPE // 2] = (key_first * cosine - key_second * sine).astype(cache_ref.dtype)
    cache_ref[:, LATENT + ROPE // 2:] = (key_first * sine + key_second * cosine).astype(cache_ref.dtype)
    kv_ref[...] = jnp.dot(latent, kvb_ref[...], preferred_element_type=jnp.float32).astype(kv_ref.dtype)


def project(normed, joined, spread, up_rows, cosine, sine, kv_gain, kvb_weight, heads):
    rows, width = normed.shape
    cols = joined.shape[1]
    half = heads * ROPE // 2
    nope = heads * NOPE
    full = lambda shape: pl.BlockSpec(shape, lambda i: (0, 0))
    part = lambda c: pl.BlockSpec((PBLOCK, c), lambda i: (i, 0))
    return pl.pallas_call(
        project_kernel,
        grid=(rows // PBLOCK,),
        in_specs=[
            part(width), full((width, cols)), part(spread.shape[1]), full(up_rows.shape),
            part(half), part(half), full((1, LATENT)), full(kvb_weight.shape),
        ],
        out_specs=[
            part(nope),
            pl.BlockSpec((heads, PBLOCK, ROPE), lambda i: (0, i, 0)),
            part(LATENT + ROPE),
            part(kvb_weight.shape[1]),
        ],
        out_shape=[
            jax.ShapeDtypeStruct((rows, nope), jnp.bfloat16),
            jax.ShapeDtypeStruct((heads, rows, ROPE), jnp.bfloat16),
            jax.ShapeDtypeStruct((rows, LATENT + ROPE), jnp.bfloat16),
            jax.ShapeDtypeStruct((rows, kvb_weight.shape[1]), jnp.bfloat16),
        ],
    )(normed, joined, spread, up_rows, cosine, sine, kv_gain.astype(jnp.float32)[None, :], kvb_weight)


def attention_kernel(me_ref, first_ref, q_nope_ref, qr_ref, kv_ref, cache_ref, kst_ref, wt_ref,
                     wm_ref, theirs_ref, mine_ref, att_ref):
    i = pl.program_id(0)
    heads = qr_ref.shape[0]
    scale = 1.0 / jnp.sqrt(jnp.float32(NOPE + ROPE))
    kst = kst_ref[...]

    def run(start, width):
        start = pl.multiple_of(start, 128)
        row = i * QBLOCK + lax.broadcasted_iota(jnp.int32, (QBLOCK, width), 0)
        col = start + lax.broadcasted_iota(jnp.int32, (QBLOCK, width), 1)
        allowed = (col >= kst) & (col <= row)
        kr = cache_ref[pl.ds(start, width), LATENT:LATENT + ROPE]
        for h in range(heads):
            qn = q_nope_ref[:, h * NOPE:(h + 1) * NOPE]
            qr = qr_ref[h]
            kn = kv_ref[pl.ds(start, width), h * (NOPE + VDIM):h * (NOPE + VDIM) + NOPE]
            s = lax.dot_general(qn, kn, (((1,), (1,)), ((), ())), preferred_element_type=jnp.float32)
            rope = lax.dot_general(qr, kr, (((1,), (1,)), ((), ())), preferred_element_type=jnp.float32)
            s = jnp.where(allowed, (s + rope) * scale, jnp.float32(-1e30))
            top = jnp.max(s, axis=1, keepdims=True)
            e = jnp.exp(s - top)
            w = (e * (1.0 / jnp.sum(e, axis=1, keepdims=True))).astype(jnp.bfloat16)
            v = kv_ref[pl.ds(start, width), h * (NOPE + VDIM) + NOPE:(h + 1) * (NOPE + VDIM)]
            att_ref[:, h * VDIM:(h + 1) * VDIM] = jnp.dot(
                w, v, preferred_element_type=jnp.float32
            ).astype(att_ref.dtype)

    first = first_ref[i]
    one = first >= i * QBLOCK
    two = jnp.logical_and(jnp.logical_not(one), first >= i * QBLOCK - QBLOCK)

    @pl.when(one)
    def _():
        run(i * QBLOCK, QBLOCK)

    @pl.when(two)
    def _():
        run(jnp.maximum(i * QBLOCK - QBLOCK, 0), 2 * QBLOCK)

    @pl.when(jnp.logical_not(jnp.logical_or(one, two)))
    def _():
        run(jnp.maximum(i * QBLOCK - LMAX, 0), WINDOW)

    att = att_ref[...]
    theirs_ref[...] = jnp.dot(att, wt_ref[...], preferred_element_type=jnp.float32).astype(theirs_ref.dtype)
    mine_ref[...] = jnp.dot(att, wm_ref[...], preferred_element_type=jnp.float32).astype(mine_ref.dtype)


def attend(me, q_nope, q_rope, kv, latent_cache, key_start, o_weight):
    rows = q_nope.shape[0]
    heads = q_nope.shape[1] // NOPE
    out_half = o_weight.shape[1] // 2
    grid_spec = pltpu.PrefetchScalarGridSpec(
        num_scalar_prefetch=2,
        grid=(rows // QBLOCK,),
        in_specs=[
            pl.BlockSpec((QBLOCK, heads * NOPE), lambda i, m, f: (i, 0)),
            pl.BlockSpec((heads, QBLOCK, ROPE), lambda i, m, f: (0, i, 0)),
            pl.BlockSpec((rows, heads * (NOPE + VDIM)), lambda i, m, f: (0, 0)),
            pl.BlockSpec((rows, LATENT + ROPE), lambda i, m, f: (0, 0)),
            pl.BlockSpec((QBLOCK, 1), lambda i, m, f: (i, 0)),
            pl.BlockSpec((heads * VDIM, out_half), lambda i, m, f: (0, 1 - m[0])),
            pl.BlockSpec((heads * VDIM, out_half), lambda i, m, f: (0, m[0])),
        ],
        out_specs=[
            pl.BlockSpec((QBLOCK, out_half), lambda i, m, f: (i, 0)),
            pl.BlockSpec((QBLOCK, out_half), lambda i, m, f: (i, 0)),
        ],
        scratch_shapes=[pltpu.VMEM((QBLOCK, heads * VDIM), jnp.bfloat16)],
    )
    return pl.pallas_call(
        attention_kernel,
        grid_spec=grid_spec,
        out_shape=[
            jax.ShapeDtypeStruct((rows, out_half), jnp.bfloat16),
            jax.ShapeDtypeStruct((rows, out_half), jnp.bfloat16),
        ],
    )(me, key_start[::QBLOCK], q_nope, q_rope, kv, latent_cache, key_start[:, None], o_weight, o_weight)


def finish_kernel(tok_ref, mine_ref, rec_ref, out_ref):
    projected = mine_ref[...].astype(jnp.float32) + rec_ref[...].astype(jnp.float32)
    out_ref[...] = (tok_ref[...].astype(jnp.float32) + projected).astype(out_ref.dtype)


def finish(tokens, mine, received):
    rows, cols = tokens.shape
    block = 512
    spec = pl.BlockSpec((block, cols), lambda i: (i, 0))
    return pl.pallas_call(
        finish_kernel,
        grid=(rows // block,),
        in_specs=[spec, spec, spec],
        out_specs=spec,
        out_shape=jax.ShapeDtypeStruct((rows, cols), tokens.dtype),
    )(tokens, mine, received)


def split_heads(weight, heads):
    parts = weight.reshape(weight.shape[0], heads, NOPE + ROPE)
    half = ROPE // 2
    return jnp.concatenate(
        [
            parts[..., :NOPE].reshape(weight.shape[0], heads * NOPE),
            parts[..., NOPE:NOPE + half].reshape(weight.shape[0], heads * half),
            parts[..., NOPE + half:].reshape(weight.shape[0], heads * half),
        ],
        axis=1,
    )


def swap(values):
    return lax.ppermute(values, "narrow", perm=[(0, 1), (1, 0)])


def body(
    tokens,
    attn_gain,
    q_weight,
    kva_weight,
    kv_gain,
    kvb_weight,
    o_weight,
    adapter_down,
    adapter_up_weight,
    lengths,
    adapter_ids,
    adapter_slot,
):
    rows = tokens.shape[0]
    half_width = tokens.shape[1]
    heads_here = o_weight.shape[0] // VDIM
    prompts_here = lengths.shape[1]
    q_cols = q_weight.shape[1]
    me = lax.axis_index("narrow")
    mine_first = me == 0

    joined = jnp.concatenate([split_heads(q_weight, heads_here), kva_weight], axis=1)
    joined = lax.all_gather(joined, "wide", axis=0, tiled=True)

    other = swap(tokens)
    whole = jnp.concatenate(
        [jnp.where(mine_first, tokens, other), jnp.where(mine_first, other, tokens)], axis=1
    )

    slots_here = adapter_down.shape[1] // RANK
    prompt_ids = adapter_ids[0]
    id_hot = (prompt_ids[:, None] == jnp.arange(adapter_slot.shape[0])[None, :]).astype(jnp.int32)
    prompt_slot = jnp.sum(id_hot * adapter_slot[None, :], axis=1)
    owner = prompt_slot // slots_here
    local_slot = prompt_slot % slots_here
    picked = jnp.concatenate(
        [
            lax.dynamic_slice_in_dim(adapter_down, local_slot[p] * RANK, RANK, 1)
            for p in range(prompts_here)
        ],
        axis=1,
    )
    picked_other = swap(picked)
    own_block = jnp.repeat(owner == me, RANK)
    chosen = jnp.where(own_block[None, :], picked, picked_other)

    normed = rms_scale(whole.astype(jnp.float32), attn_gain).astype(jnp.bfloat16)
    local_pos = jnp.arange(rows)
    prompt, position, adapter, slot = token_tables(
        lengths[0], adapter_ids[0], adapter_slot, local_pos
    )
    member = (prompt[:, None] == jnp.arange(prompts_here)[None, :]).astype(jnp.float32)
    low = jnp.dot(normed, chosen, preferred_element_type=jnp.float32).reshape(
        rows, prompts_here, RANK
    )
    lowrank = jnp.sum(low * member[:, :, None], axis=1).astype(jnp.bfloat16)
    up_blocks = [
        lax.dynamic_slice_in_dim(adapter_up_weight, prompt_ids[prompt_index] * RANK, RANK, 0)
        for prompt_index in range(prompts_here)
    ]
    up_weight_rows = split_heads(jnp.concatenate(up_blocks, axis=0), heads_here)
    spread_rows = (member.astype(jnp.bfloat16)[:, :, None] * lowrank[:, None, :]).reshape(
        rows, prompts_here * RANK
    )
    half = ROPE // 2
    freqs = jnp.exp(-jnp.log(THETA) * 2.0 * jnp.arange(half).astype(jnp.float32) / (2 * half))
    angle = position.astype(jnp.float32)[:, None] * freqs[None, :]
    cosine = jnp.tile(jnp.cos(angle), (1, heads_here))
    sine = jnp.tile(jnp.sin(angle), (1, heads_here))
    q_nope, q_rope, latent_cache, expanded = project(
        normed, joined, spread_rows, up_weight_rows, cosine, sine, kv_gain, kvb_weight, heads_here
    )
    key_start = (local_pos - position).astype(jnp.int32)
    theirs, mine = attend(
        me.astype(jnp.int32).reshape(1), q_nope, q_rope, expanded, latent_cache,
        key_start, o_weight,
    )
    received = swap(theirs)
    hidden = finish(tokens, mine, received)
    return (hidden, latent_cache)


def solution(mesh):
    return jax.shard_map(
        body,
        mesh=mesh,
        in_specs=(
            P("wide", "narrow"),
            P(),
            P("wide", "narrow"),
            P("wide", None),
            P(),
            P(None, "narrow"),
            P("narrow", None),
            P(None, "narrow"),
            P(None, "narrow"),
            P("wide", None),
            P("wide", None),
            P(),
        ),
        out_specs=(P("wide", "narrow"), P("wide", None)),
        check_vma=False,
    )
```
